32 devices in a mesh: sample: 16 (over z, x, core), block: 2 (over y).
Axes of the slice: x: 2, y: 2, z: 4, core: 2. Of those that a mesh axis runs over, the one named last changes fastest.
Arguments:
- genotype: int32 [16384, 2000], P('sample', 'block'), may hold values from 0 to 2
- allele_freq: float32 [2000], P('block'), may hold values from 0.05 to 0.5
- phenotype: bfloat16 [16384, 16], P('sample'), may hold values from -6 to 6
- shrinkage: float32 [2], replicated, may hold values from 0.05 to 2
- owner_order: int32 [16], replicated, may hold values from 0 to 15, each once
Outputs:
- predictions: bfloat16 [16, 8, 16384], P('block', None, 'sample')
The draws below stay inside these ranges and needn't reach their ends.
Inputs may be any that keep to these rules, and one draw needn't show every extreme that they name: `owner_order`: each phenotype appears once.
All inputs are finite; a program needn't handle non-finite values.
Results may differ from the reference program's by a relative error of at most 0.0056.
Values may be sent and summed in bfloat16 or wider, within the bound.
No kernel may reach another device: no remote copies, remote signals or barrier semaphores. Data moves between devices by JAX's collectives and lax.ppermute only.
A program may use at most 128 MiB of HBM per device.

```python
import jax
import jax.numpy as jnp
from jax import lax

SNPS = 500
PHENOS = 16
RIDGES = 2
FOLDS = 5
TOTAL_SAMPLES = 16384
BLOCKS = 4
SNP_TOTAL = 2000


def cohort(key):
    percent = jax.random.randint(jax.random.fold_in(key, 11), (SNP_TOTAL,), 5, 51)
    percent = percent.at[0].set(5).at[1].set(50)
    weight_key = jax.random.fold_in(key, 13)

    def one_block(column):
        block_key = jax.random.fold_in(jax.random.fold_in(key, 17), column)
        offset = (column * SNPS).astype(jnp.int32)
        cutoff = lax.dynamic_slice_in_dim(percent, offset, SNPS)
        positions = lax.broadcasted_iota(jnp.int32, (TOTAL_SAMPLES, SNPS), 1)
        dosage = jnp.zeros((TOTAL_SAMPLES, SNPS), jnp.int32)
        for strand in range(2):
            strand_key = jax.random.fold_in(block_key, strand)
            renewed = jax.random.randint(jax.random.fold_in(strand_key, 1), (TOTAL_SAMPLES, SNPS), 0, 64) == 0
            renewed = jnp.logical_or(renewed, positions == 0)
            anchor = lax.cummax(jnp.where(renewed, positions, 0), axis=1)
            ticket = jax.random.randint(jax.random.fold_in(strand_key, 2), (TOTAL_SAMPLES, SNPS), 0, 100)
            carried = jnp.take_along_axis(ticket, anchor, axis=1)
            dosage = dosage + (carried < cutoff[None, :]).astype(jnp.int32)
        frequency = cutoff.astype(jnp.float32) / 100.0
        scaled = (dosage.astype(jnp.float32) - 2.0 * frequency) / jnp.sqrt(2.0 * frequency * (1.0 - frequency))
        effect = jax.random.normal(jax.random.fold_in(weight_key, column), (SNPS, PHENOS), jnp.float32)
        return (dosage, jnp.dot(scaled, effect, precision=lax.Precision.HIGHEST))
    dosages, shares = lax.map(one_block, jnp.arange(BLOCKS, dtype=jnp.int32))
    genetic = jnp.sum(shares, axis=0)
    genotype = jnp.transpose(dosages, (1, 0, 2)).reshape(TOTAL_SAMPLES, SNP_TOTAL)
    return (genotype, percent, genetic)


def draw_genotype(key, part):
    return cohort(key)[0]


def draw_allele_freq(key, part):
    return cohort(key)[1].astype(jnp.float32) / 100.0


def draw_phenotype(key, part):
    genetic = cohort(key)[2]
    centered = genetic - jnp.mean(genetic, axis=0)
    spread = jnp.sqrt(jnp.mean(centered * centered, axis=0))
    signal = centered / spread
    residue_key = jax.random.fold_in(key, 19)
    herit_key = jax.random.fold_in(key, 23)
    heritable = jax.random.uniform(herit_key, (PHENOS,), jnp.float32, 0.3, 0.8)
    residue = jax.random.normal(residue_key, (TOTAL_SAMPLES, PHENOS), jnp.float32)
    traits = jnp.sqrt(heritable) * signal + jnp.sqrt(1.0 - heritable) * residue
    return jnp.clip(traits, -6.0, 6.0).astype(jnp.bfloat16)


def draw_shrinkage(key, part):
    fraction = jax.random.uniform(jax.random.fold_in(key, 31), (2,), jnp.float32, 0.0, 1.0)
    small_lo, small_hi, large_lo, large_hi = (0.05, 0.08, 0.5, 2.0)
    small_value = small_lo * jnp.exp(fraction[0] * jnp.log(small_hi / small_lo))
    large_value = large_lo * jnp.exp(fraction[1] * jnp.log(large_hi / large_lo))
    flip = jax.random.randint(jax.random.fold_in(key, 37), (), 0, 2)
    first = jnp.where(flip == 1, large_value, small_value)
    second = jnp.where(flip == 1, small_value, large_value)
    return jnp.clip(jnp.stack([first, second]), 0.05, 2.0).astype(jnp.float32)


def setup_inputs(seed: int = 0) -> dict:
    key_list = jax.random.split(jax.random.key(seed), 6)
    return {
        "genotype": draw_genotype(jax.random.fold_in(key_list[5], 71), 0),
        "allele_freq": draw_allele_freq(jax.random.fold_in(key_list[5], 71), 0),
        "phenotype": draw_phenotype(jax.random.fold_in(key_list[5], 71), 0),
        "shrinkage": draw_shrinkage(jax.random.fold_in(key_list[5], 71), 0),
        "owner_order": jax.random.permutation(key_list[4], PHENOS).astype(jnp.int32),
    }


def standardize(genotype, allele_freq):
    spread = jnp.sqrt(2.0 * allele_freq * (1.0 - allele_freq))
    return ((genotype.astype(jnp.float32) - 2.0 * allele_freq) / spread).astype(jnp.bfloat16)

def solve_pair(factor, target):
    return jax.scipy.linalg.cho_solve((factor, True), target)

def ridge_solve(grams, crosses, shrinkage, counts):
    lead = grams.shape[:2]
    width = grams.shape[-1]
    system = grams / counts[:, None, None, None]
    target = crosses / counts[:, None, None, None]
    system = system.reshape(-1, width, width)
    target = target.reshape(-1, width, crosses.shape[-1])
    identity = jnp.eye(width, dtype=jnp.float32)
    full = system[:, None] + shrinkage[None, :, None, None] * identity
    factor = jnp.linalg.cholesky(full)
    per_ridge = jax.vmap(solve_pair, (0, None))
    solved = jax.vmap(per_ridge, (0, 0))(factor, target)
    return solved.reshape(lead + solved.shape[1:])

def predict(columns, weights):
    stacked = jnp.transpose(weights, (2, 0, 1)).reshape(-1, weights.shape[1])
    product = lax.dot_general(stacked.astype(jnp.float32), columns.astype(jnp.float32), (((1,), (1,)), ((), ())), preferred_element_type=jnp.float32)
    return product.astype(jnp.bfloat16).reshape(weights.shape[2], weights.shape[0], columns.shape[0])

def fold_bounds(total):
    return [-(-(k * total) // FOLDS) for k in range(FOLDS + 1)]

def reference(genotype, allele_freq, phenotype, shrinkage, owner_order):
    scaled = standardize(genotype, allele_freq)
    ordered = jnp.take(phenotype, owner_order, axis=1)
    bounds = fold_bounds(TOTAL_SAMPLES)
    sizes_list = [float(TOTAL_SAMPLES - (bounds[k + 1] - bounds[k])) for k in range(FOLDS)]
    counts = jnp.array(sizes_list, dtype=jnp.float32)

    def block_sums(column):
        offset = (column * SNPS).astype(jnp.int32)
        columns = lax.dynamic_slice_in_dim(scaled, offset, SNPS, 1)
        gram_list = []
        cross_list = []
        for k in range(FOLDS):
            part_cols = columns[bounds[k]:bounds[k + 1]]
            part_traits = ordered[bounds[k]:bounds[k + 1]]
            gram_list.append(lax.dot_general(part_cols.astype(jnp.float32), part_cols.astype(jnp.float32), (((0,), (0,)), ((), ())), preferred_element_type=jnp.float32))
            cross_list.append(lax.dot_general(part_cols.astype(jnp.float32), part_traits.astype(jnp.float32), (((0,), (0,)), ((), ())), preferred_element_type=jnp.float32))
        return (jnp.stack(gram_list), jnp.stack(cross_list))
    grams, crosses = lax.map(block_sums, jnp.arange(BLOCKS, dtype=jnp.int32))
    grams = jnp.transpose(grams, (1, 0, 2, 3))
    crosses = jnp.transpose(crosses, (1, 0, 2, 3))
    rest_grams = lax.optimization_barrier(jnp.sum(grams, axis=0))[None] - grams
    rest_crosses = lax.optimization_barrier(jnp.sum(crosses, axis=0))[None] - crosses
    weights = ridge_solve(rest_grams, rest_crosses, shrinkage, counts).astype(jnp.bfloat16)
    weights = jnp.transpose(weights, (1, 0, 2, 3, 4))

    def block_predictions(packed):
        column, block_weights = packed
        offset = (column * SNPS).astype(jnp.int32)
        columns = lax.dynamic_slice_in_dim(scaled, offset, SNPS, 1)
        pieces = [predict(columns[bounds[k]:bounds[k + 1]], block_weights[k]) for k in range(FOLDS)]
        return jnp.concatenate(pieces, axis=2)
    predictions = lax.map(block_predictions, (jnp.arange(BLOCKS, dtype=jnp.int32), weights))
    return jnp.transpose(predictions, (1, 0, 2, 3)).reshape(PHENOS, BLOCKS * RIDGES, TOTAL_SAMPLES)
```

```python
import jax
import jax.numpy as jnp
from jax import lax
from jax.sharding import PartitionSpec as P

SNPS = 500
FOLDS = 5
PANEL = 128
HIGH = lax.Precision.HIGHEST


def standardize(genotype, allele_freq):
    spread = jnp.sqrt(2.0 * allele_freq * (1.0 - allele_freq))
    return ((genotype.astype(jnp.float32) - 2.0 * allele_freq) / spread).astype(jnp.bfloat16)


def predict(columns, weights):
    stacked = jnp.transpose(weights, (2, 0, 1)).reshape(-1, weights.shape[1])
    product = lax.dot_general(
        stacked, columns, (((1,), (1,)), ((), ())), preferred_element_type=jnp.float32
    )
    return product.astype(jnp.bfloat16).reshape(
        weights.shape[2], weights.shape[0], columns.shape[0]
    )


def inner_products(left_cols, right_cols):
    return lax.dot_general(
        left_cols, right_cols, (((0,), (0,)), ((), ())), preferred_element_type=jnp.float32
    )


def tile_pairs(panels):
    pairs = []
    for row_tile in range(panels):
        for col_tile in range(row_tile, panels):
            pairs.append((row_tile, col_tile))
    return pairs


def tile_grams(left_cols, right_cols, panels):
    tile_list = []
    for row_tile, col_tile in tile_pairs(panels):
        first = left_cols[:, row_tile * PANEL : (row_tile + 1) * PANEL]
        second = right_cols[:, col_tile * PANEL : (col_tile + 1) * PANEL]
        tile_list.append(inner_products(first, second))
    return jnp.stack(tile_list)


def mm(spec, left, right):
    return jnp.einsum(spec, left, right, precision=HIGH, preferred_element_type=jnp.float32)


def block_solve(tiles, target, panels):
    pairs = tile_pairs(panels)
    upper = {pair: tiles[:, index] for index, pair in enumerate(pairs)}
    eye = jnp.broadcast_to(jnp.eye(PANEL, dtype=jnp.float32), (tiles.shape[0], PANEL, PANEL))
    lower = {}
    inverse = {}
    for p in range(panels):
        factor = jnp.linalg.cholesky(upper[(p, p)])
        inv = lax.linalg.triangular_solve(factor, eye, left_side=True, lower=True)
        inverse[p] = inv
        for q in range(p + 1, panels):
            lower[(q, p)] = mm("sji,skj->sik", upper[(p, q)], inv)
        for r in range(p + 1, panels):
            for q in range(r, panels):
                upper[(r, q)] = upper[(r, q)] - mm("sik,sjk->sij", lower[(r, p)], lower[(q, p)])
    forward = []
    for p in range(panels):
        rhs = target[:, p * PANEL : (p + 1) * PANEL]
        for q in range(p):
            rhs = rhs - mm("sij,sjc->sic", lower[(p, q)], forward[q])
        forward.append(mm("sij,sjc->sic", inverse[p], rhs))
    backward = [None] * panels
    for p in reversed(range(panels)):
        rhs = forward[p]
        for q in range(p + 1, panels):
            rhs = rhs - mm("sji,sjc->sic", lower[(q, p)], backward[q])
        backward[p] = mm("sji,sjc->sic", inverse[p], rhs)
    return jnp.concatenate(backward, axis=1)


def shared_solve(summed_grams, summed_crosses, shrinkage, counts, panels):
    member_count = summed_grams.shape[1]
    ridge_count = shrinkage.shape[0]
    systems = FOLDS * member_count * ridge_count
    devices = lax.axis_size("sample")
    share = -(-systems // devices)
    owned_ids = lax.axis_index("sample") * share + lax.broadcasted_iota(jnp.int32, (share,), 0)
    owned_ids = jnp.minimum(owned_ids, systems - 1)
    pair_ids = owned_ids // ridge_count
    ridge_ids = owned_ids % ridge_count
    fold_ids = pair_ids // member_count
    member_ids = pair_ids % member_count
    fold_axis = jnp.arange(FOLDS, dtype=jnp.int32)[:, None, None]
    member_axis = jnp.arange(member_count, dtype=jnp.int32)[None, :, None]
    keep = jnp.logical_and(fold_axis != fold_ids[None, None, :], member_axis == member_ids[None, None, :])
    keep = keep.astype(jnp.float32)
    rest_tiles = jnp.einsum("kms,kmtij->stij", keep, summed_grams, precision=HIGH)
    rest_crosses = jnp.einsum("kms,kmic->sic", keep, summed_crosses, precision=HIGH)
    chosen_counts = jnp.take(counts, fold_ids, axis=0)
    ridge = jnp.take(shrinkage, ridge_ids, axis=0)
    width = rest_tiles.shape[-1]
    diag_ids = [index for index, (row_tile, col_tile) in enumerate(tile_pairs(panels)) if row_tile == col_tile]
    is_diag = jnp.zeros((len(tile_pairs(panels)),), jnp.float32).at[jnp.array(diag_ids)].set(1.0)
    position = lax.broadcasted_iota(jnp.int32, (panels, width), 1) + PANEL * lax.broadcasted_iota(
        jnp.int32, (panels, width), 0
    )
    padded = (position >= SNPS).astype(jnp.float32)
    pad_diag = jnp.zeros((len(tile_pairs(panels)), width), jnp.float32).at[jnp.array(diag_ids)].set(padded)
    identity = jnp.eye(width, dtype=jnp.float32)
    diag_add = (
        ridge[:, None, None] * is_diag[None, :, None]
        + (1.0 - ridge[:, None, None]) * pad_diag[None, :, :]
    )
    system = rest_tiles / chosen_counts[:, None, None, None] + diag_add[:, :, :, None] * identity
    target = rest_crosses / chosen_counts[:, None, None]
    solved = block_solve(system, target, panels)[:, :SNPS].astype(jnp.bfloat16)
    collected = lax.all_gather(solved, "sample", axis=0, tiled=True)
    return collected[:systems].reshape(FOLDS, member_count, ridge_count, SNPS, -1)


def shards(genotype, allele_freq, phenotype, shrinkage, owner_order):
    sample_rows = genotype.shape[0]
    total_rows = sample_rows * lax.axis_size("sample")
    scaled = standardize(genotype, allele_freq)
    ordered = jnp.take(phenotype, owner_order, axis=1)
    local_blocks = allele_freq.shape[0] // SNPS
    panels = -(-SNPS // PANEL)
    padded_width = panels * PANEL
    column_sets = [scaled[:, member * SNPS : (member + 1) * SNPS] for member in range(local_blocks)]
    bounds = [-(-(k * total_rows) // FOLDS) for k in range(FOLDS + 1)]
    counts = jnp.array(
        [float(total_rows - (bounds[k + 1] - bounds[k])) for k in range(FOLDS)], dtype=jnp.float32
    )
    start_row = lax.axis_index("sample") * sample_rows
    row_ids = start_row + lax.broadcasted_iota(jnp.int32, (sample_rows,), 0)
    fold_of = row_ids * FOLDS // total_rows
    first_fold = start_row * FOLDS // total_rows
    slot_folds = [first_fold, first_fold + 1]
    slot_masks = [fold_of == slot_folds[0], fold_of == slot_folds[1]]
    picked = jnp.minimum(jnp.stack(slot_folds), FOLDS - 1)
    fold_ids = jnp.arange(FOLDS, dtype=jnp.int32)
    tile_count = len(tile_pairs(panels))

    def fold_partials(member):
        columns = jnp.pad(column_sets[member], ((0, 0), (0, padded_width - SNPS)))
        gram_total = jnp.zeros((FOLDS, tile_count, PANEL, PANEL), jnp.float32)
        cross_total = jnp.zeros((FOLDS, padded_width, ordered.shape[1]), jnp.float32)
        for slot in range(2):
            masked = jnp.where(slot_masks[slot][:, None], columns, jnp.zeros_like(columns))
            selector = (fold_ids == slot_folds[slot]).astype(jnp.float32)
            gram_total = (
                gram_total
                + selector[:, None, None, None] * tile_grams(masked, columns, panels)[None]
            )
            cross_total = (
                cross_total + selector[:, None, None] * inner_products(masked, ordered)[None]
            )
        return (gram_total, cross_total)

    def weights_for(members):
        parts = [fold_partials(member) for member in members]
        grams = jnp.stack([item[0] for item in parts], axis=1)
        crosses = jnp.stack([item[1] for item in parts], axis=1)
        summed_grams, summed_crosses = lax.psum((grams, crosses), "sample")
        every_weights = shared_solve(summed_grams, summed_crosses, shrinkage, counts, panels)
        return jnp.take(every_weights, picked, axis=0)

    def fold_predictions(member, slot_weights):
        columns = column_sets[member]
        lower = predict(columns, slot_weights[0])
        upper = predict(columns, slot_weights[1])
        return jnp.where(slot_masks[1][None, None, :], upper, lower)

    weights = weights_for(list(range(local_blocks)))
    local_preds = jnp.concatenate(
        [fold_predictions(member, weights[:, member]) for member in range(local_blocks)], axis=1
    )
    return lax.all_to_all(local_preds, "block", split_axis=0, concat_axis=1, tiled=True)


def solution(mesh):
    in_specs = (P("sample", "block"), P("block"), P("sample", None), P(), P())
    out_specs = P("block", None, "sample")
    return jax.shard_map(shards, mesh=mesh, in_specs=in_specs, out_specs=out_specs, check_vma=False)
```

```python
import jax
import jax.numpy as jnp
from jax import lax
from jax.sharding import PartitionSpec as P

SNPS = 500
FOLDS = 5
PANEL = 128
HIGH = lax.Precision.HIGHEST


def standardize(genotype, allele_freq):
    spread = jnp.sqrt(2.0 * allele_freq * (1.0 - allele_freq))
    return ((genotype.astype(jnp.float32) - 2.0 * allele_freq) / spread).astype(jnp.bfloat16)


def predict(columns, weights):
    stacked = jnp.transpose(weights, (2, 0, 1)).reshape(-1, weights.shape[1])
    product = lax.dot_general(
        stacked, columns, (((1,), (1,)), ((), ())), preferred_element_type=jnp.float32
    )
    return product.astype(jnp.bfloat16).reshape(
        weights.shape[2], weights.shape[0], columns.shape[0]
    )


def inner_products(left_cols, right_cols):
    return lax.dot_general(
        left_cols, right_cols, (((0,), (0,)), ((), ())), preferred_element_type=jnp.float32
    )


def tile_pairs(panels):
    pairs = []
    for row_tile in range(panels):
        for col_tile in range(row_tile, panels):
            pairs.append((row_tile, col_tile))
    return pairs


def tile_grams(left_cols, right_cols, panels):
    tile_list = []
    for row_tile, col_tile in tile_pairs(panels):
        first = left_cols[:, row_tile * PANEL : (row_tile + 1) * PANEL]
        second = right_cols[:, col_tile * PANEL : (col_tile + 1) * PANEL]
        tile_list.append(inner_products(first, second))
    return jnp.stack(tile_list)


def mm(spec, left, right):
    return jnp.einsum(spec, left, right, precision=HIGH, preferred_element_type=jnp.float32)


def block_solve(tiles, target, panels):
    pairs = tile_pairs(panels)
    upper = {pair: tiles[:, index] for index, pair in enumerate(pairs)}
    eye = jnp.broadcast_to(jnp.eye(PANEL, dtype=jnp.float32), (tiles.shape[0], PANEL, PANEL))
    lower = {}
    inverse = {}
    for p in range(panels):
        factor = jnp.linalg.cholesky(upper[(p, p)])
        inv = lax.linalg.triangular_solve(factor, eye, left_side=True, lower=True)
        inverse[p] = inv
        for q in range(p + 1, panels):
            lower[(q, p)] = mm("sji,skj->sik", upper[(p, q)], inv)
        for r in range(p + 1, panels):
            for q in range(r, panels):
                upper[(r, q)] = upper[(r, q)] - mm("sik,sjk->sij", lower[(r, p)], lower[(q, p)])
    forward = []
    for p in range(panels):
        rhs = target[:, p * PANEL : (p + 1) * PANEL]
        for q in range(p):
            rhs = rhs - mm("sij,sjc->sic", lower[(p, q)], forward[q])
        forward.append(mm("sij,sjc->sic", inverse[p], rhs))
    backward = [None] * panels
    for p in reversed(range(panels)):
        rhs = forward[p]
        for q in range(p + 1, panels):
            rhs = rhs - mm("sji,sjc->sic", lower[(q, p)], backward[q])
        backward[p] = mm("sji,sjc->sic", inverse[p], rhs)
    return jnp.concatenate(backward, axis=1)


def owned_layout(systems, devices, ridge_count):
    share = -(-systems // devices)
    firsts = []
    spans = []
    for device in range(devices):
        first = min(device * share, systems - 1) // ridge_count
        last = min(device * share + share - 1, systems - 1) // ridge_count
        firsts.append(first)
        spans.append(last - first + 1)
    return share, firsts, max(spans)


def shards(genotype, allele_freq, phenotype, shrinkage, owner_order):
    sample_rows = genotype.shape[0]
    devices = lax.axis_size("sample")
    me = lax.axis_index("sample")
    total_rows = sample_rows * devices
    scaled = standardize(genotype, allele_freq)
    ordered = jnp.take(phenotype, owner_order, axis=1)
    traits = ordered.shape[1]
    member_count = allele_freq.shape[0] // SNPS
    ridge_count = shrinkage.shape[0]
    panels = -(-SNPS // PANEL)
    padded_width = panels * PANEL
    tile_count = len(tile_pairs(panels))
    pair_count = FOLDS * member_count
    systems = pair_count * ridge_count
    share, firsts, span = owned_layout(systems, devices, ridge_count)
    column_sets = [scaled[:, member * SNPS : (member + 1) * SNPS] for member in range(member_count)]
    bounds = [-(-(k * total_rows) // FOLDS) for k in range(FOLDS + 1)]
    counts = jnp.array(
        [float(total_rows - (bounds[k + 1] - bounds[k])) for k in range(FOLDS)], dtype=jnp.float32
    )
    start_row = me * sample_rows
    row_ids = start_row + lax.broadcasted_iota(jnp.int32, (sample_rows,), 0)
    fold_of = row_ids * FOLDS // total_rows
    first_fold = start_row * FOLDS // total_rows
    slot_folds = [first_fold, first_fold + 1]
    slot_masks = [fold_of == slot_folds[0], fold_of == slot_folds[1]]
    picked = jnp.minimum(jnp.stack(slot_folds), FOLDS - 1)

    gram_parts = []
    cross_parts = []
    for member in range(member_count):
        columns = jnp.pad(column_sets[member], ((0, 0), (0, padded_width - SNPS)))
        slot_grams = []
        slot_crosses = []
        for slot in range(2):
            masked = jnp.where(slot_masks[slot][:, None], columns, jnp.zeros_like(columns))
            slot_grams.append(tile_grams(masked, columns, panels))
            slot_crosses.append(inner_products(masked, ordered))
        gram_parts.append(jnp.stack(slot_grams))
        cross_parts.append(jnp.stack(slot_crosses))
    local_grams = jnp.stack(gram_parts, axis=1)
    local_crosses = jnp.stack(cross_parts, axis=1)

    wanted = []
    for device in range(devices):
        for offset in range(span):
            wanted.append(min(firsts[device] + offset, pair_count - 1))
    wanted_folds = jnp.array([pair // member_count for pair in wanted], jnp.int32)
    wanted_members = jnp.array([pair % member_count for pair in wanted], jnp.int32)
    member_axis = jnp.arange(member_count, dtype=jnp.int32)
    coefficient = jnp.stack(
        [
            jnp.logical_and(wanted_folds[:, None] != slot_folds[slot], wanted_members[:, None] == member_axis[None, :])
            for slot in range(2)
        ],
        axis=1,
    ).astype(jnp.float32)
    gram_payload = jnp.einsum("wjm,jmtab->wtab", coefficient, local_grams, precision=HIGH)
    cross_payload = jnp.einsum("wjm,jmic->wic", coefficient, local_crosses, precision=HIGH)
    gram_rows = gram_payload.reshape(devices, span * tile_count * PANEL, PANEL)
    cross_rows = cross_payload.reshape(devices, span * padded_width * traits // PANEL, PANEL)
    payload = jnp.concatenate([gram_rows, cross_rows], axis=1)
    reduced = lax.psum_scatter(payload, "sample", scatter_dimension=0, tiled=True)[0]
    split = span * tile_count * PANEL
    mine_grams = reduced[:split].reshape(span, tile_count, PANEL, PANEL)
    mine_crosses = reduced[split:].reshape(span, padded_width, traits)

    owned_ids = jnp.minimum(me * share + lax.broadcasted_iota(jnp.int32, (share,), 0), systems - 1)
    pair_ids = owned_ids // ridge_count
    ridge_ids = owned_ids % ridge_count
    local_ids = pair_ids - jnp.take(jnp.array(firsts, jnp.int32), me)
    rest_tiles = jnp.take(mine_grams, local_ids, axis=0)
    rest_crosses = jnp.take(mine_crosses, local_ids, axis=0)
    chosen_counts = jnp.take(counts, pair_ids // member_count, axis=0)
    ridge = jnp.take(shrinkage, ridge_ids, axis=0)
    diag_ids = [index for index, (row_tile, col_tile) in enumerate(tile_pairs(panels)) if row_tile == col_tile]
    is_diag = jnp.zeros((tile_count,), jnp.float32).at[jnp.array(diag_ids)].set(1.0)
    position = lax.broadcasted_iota(jnp.int32, (panels, PANEL), 1) + PANEL * lax.broadcasted_iota(
        jnp.int32, (panels, PANEL), 0
    )
    padded = (position >= SNPS).astype(jnp.float32)
    pad_diag = jnp.zeros((tile_count, PANEL), jnp.float32).at[jnp.array(diag_ids)].set(padded)
    identity = jnp.eye(PANEL, dtype=jnp.float32)
    diag_add = (
        ridge[:, None, None] * is_diag[None, :, None]
        + (1.0 - ridge[:, None, None]) * pad_diag[None, :, :]
    )
    system = rest_tiles / chosen_counts[:, None, None, None] + diag_add[:, :, :, None] * identity
    target = rest_crosses / chosen_counts[:, None, None]
    solved = block_solve(system, target, panels)[:, :SNPS].astype(jnp.bfloat16)
    collected = lax.all_gather(solved, "sample", axis=0, tiled=True)
    every_weights = collected[:systems].reshape(FOLDS, member_count, ridge_count, SNPS, traits)
    weights = jnp.take(every_weights, picked, axis=0)

    def fold_predictions(member, slot_weights):
        columns = column_sets[member]
        lower = predict(columns, slot_weights[0])
        upper = predict(columns, slot_weights[1])
        return jnp.where(slot_masks[1][None, None, :], upper, lower)

    local_preds = jnp.concatenate(
        [fold_predictions(member, weights[:, member]) for member in range(member_count)], axis=1
    )
    return lax.all_to_all(local_preds, "block", split_axis=0, concat_axis=1, tiled=True)


def solution(mesh):
    in_specs = (P("sample", "block"), P("block"), P("sample", None), P(), P())
    out_specs = P("block", None, "sample")
    return jax.shard_map(shards, mesh=mesh, in_specs=in_specs, out_specs=out_specs, check_vma=False)
```

```python
import jax
import jax.numpy as jnp
from jax import lax
from jax.experimental import pallas as pl
from jax.experimental.pallas import tpu as pltpu
from jax.sharding import PartitionSpec as P

SNPS = 500
FOLDS = 5
PANEL = 128
HIGH = lax.Precision.HIGHEST


def standardize(genotype, allele_freq):
    spread = jnp.sqrt(2.0 * allele_freq * (1.0 - allele_freq))
    return ((genotype.astype(jnp.float32) - 2.0 * allele_freq) / spread).astype(jnp.bfloat16)


def predict(columns, weights):
    stacked = jnp.transpose(weights, (2, 0, 1)).reshape(-1, weights.shape[1])
    product = lax.dot_general(
        stacked, columns, (((1,), (1,)), ((), ())), preferred_element_type=jnp.float32
    )
    return product.astype(jnp.bfloat16).reshape(
        weights.shape[2], weights.shape[0], columns.shape[0]
    )


def inner_products(left_cols, right_cols):
    return lax.dot_general(
        left_cols, right_cols, (((0,), (0,)), ((), ())), preferred_element_type=jnp.float32
    )


def tile_pairs(panels):
    pairs = []
    for row_tile in range(panels):
        for col_tile in range(row_tile, panels):
            pairs.append((row_tile, col_tile))
    return pairs


def tile_grams(left_cols, right_cols, panels):
    tile_list = []
    for row_tile, col_tile in tile_pairs(panels):
        first = left_cols[:, row_tile * PANEL : (row_tile + 1) * PANEL]
        second = right_cols[:, col_tile * PANEL : (col_tile + 1) * PANEL]
        tile_list.append(inner_products(first, second))
    return jnp.stack(tile_list)


def mm(spec, left, right):
    return jnp.einsum(spec, left, right, precision=HIGH, preferred_element_type=jnp.float32)


def inverse_factor_kernel(d_ref, w_ref, a_scr):
    count, n, _ = d_ref.shape
    a_scr[...] = d_ref[...]
    sub = lax.broadcasted_iota(jnp.int32, (n, n), 0)
    lane = lax.broadcasted_iota(jnp.int32, (n, n), 1)
    eye = jnp.where(sub == lane, 1.0, 0.0).astype(jnp.float32)
    for s in range(count):
        w_ref[s] = eye
    row_lane = lax.broadcasted_iota(jnp.int32, (1, n), 1)
    col_sub = lax.broadcasted_iota(jnp.int32, (n, 1), 0)

    def step(j, carry):
        for s in range(count):
            a = a_scr[s]
            row = jnp.sum(jnp.where(sub == j, a, 0.0), axis=0, keepdims=True)
            piv = jnp.sum(jnp.where(row_lane == j, row, 0.0), axis=1, keepdims=True)
            scale = 1.0 / jnp.sqrt(piv)
            col = jnp.sum(jnp.where(lane == j, a, 0.0), axis=1, keepdims=True)
            lcol = jnp.where(col_sub >= j, col * scale, 0.0)
            lrow = jnp.where(row_lane >= j, row * scale, 0.0)
            a_scr[s] = a - lcol * lrow
            r = w_ref[s]
            xrow = jnp.sum(jnp.where(sub == j, r, 0.0), axis=0, keepdims=True) * scale
            strict = jnp.where(col_sub > j, lcol, 0.0)
            w_ref[s] = jnp.where(sub == j, xrow, r - strict * xrow)
        return carry

    lax.fori_loop(0, n, step, 0)


def inverse_factor(block):
    count, n, _ = block.shape
    return pl.pallas_call(
        inverse_factor_kernel,
        out_shape=jax.ShapeDtypeStruct(block.shape, jnp.float32),
        in_specs=[pl.BlockSpec(memory_space=pltpu.VMEM)],
        out_specs=pl.BlockSpec(memory_space=pltpu.VMEM),
        scratch_shapes=[pltpu.VMEM(block.shape, jnp.float32)],
        cost_estimate=pl.CostEstimate(
            flops=12 * count * n * n * n, bytes_accessed=8 * count * n * n, transcendentals=count * n
        ),
    )(block)


def block_solve(tiles, target, panels):
    pairs = tile_pairs(panels)
    upper = {pair: tiles[:, index] for index, pair in enumerate(pairs)}
    lower = {}
    inverse = {}
    for p in range(panels):
        inv = inverse_factor(upper[(p, p)])
        inverse[p] = inv
        for q in range(p + 1, panels):
            lower[(q, p)] = mm("sji,skj->sik", upper[(p, q)], inv)
        for r in range(p + 1, panels):
            for q in range(r, panels):
                upper[(r, q)] = upper[(r, q)] - mm("sik,sjk->sij", lower[(r, p)], lower[(q, p)])
    forward = []
    for p in range(panels):
        rhs = target[:, p * PANEL : (p + 1) * PANEL]
        for q in range(p):
            rhs = rhs - mm("sij,sjc->sic", lower[(p, q)], forward[q])
        forward.append(mm("sij,sjc->sic", inverse[p], rhs))
    backward = [None] * panels
    for p in reversed(range(panels)):
        rhs = forward[p]
        for q in range(p + 1, panels):
            rhs = rhs - mm("sji,sjc->sic", lower[(q, p)], backward[q])
        backward[p] = mm("sji,sjc->sic", inverse[p], rhs)
    return jnp.concatenate(backward, axis=1)


def owned_layout(systems, devices, ridge_count):
    share = -(-systems // devices)
    firsts = []
    spans = []
    for device in range(devices):
        first = min(device * share, systems - 1) // ridge_count
        last = min(device * share + share - 1, systems - 1) // ridge_count
        firsts.append(first)
        spans.append(last - first + 1)
    return share, firsts, max(spans)


def shards(genotype, allele_freq, phenotype, shrinkage, owner_order):
    sample_rows = genotype.shape[0]
    devices = lax.axis_size("sample")
    me = lax.axis_index("sample")
    total_rows = sample_rows * devices
    scaled = standardize(genotype, allele_freq)
    ordered = jnp.take(phenotype, owner_order, axis=1)
    traits = ordered.shape[1]
    member_count = allele_freq.shape[0] // SNPS
    ridge_count = shrinkage.shape[0]
    panels = -(-SNPS // PANEL)
    padded_width = panels * PANEL
    tile_count = len(tile_pairs(panels))
    pair_count = FOLDS * member_count
    systems = pair_count * ridge_count
    share, firsts, span = owned_layout(systems, devices, ridge_count)
    column_sets = [scaled[:, member * SNPS : (member + 1) * SNPS] for member in range(member_count)]
    bounds = [-(-(k * total_rows) // FOLDS) for k in range(FOLDS + 1)]
    counts = jnp.array(
        [float(total_rows - (bounds[k + 1] - bounds[k])) for k in range(FOLDS)], dtype=jnp.float32
    )
    start_row = me * sample_rows
    row_ids = start_row + lax.broadcasted_iota(jnp.int32, (sample_rows,), 0)
    fold_of = row_ids * FOLDS // total_rows
    first_fold = start_row * FOLDS // total_rows
    slot_folds = [first_fold, first_fold + 1]
    slot_masks = [fold_of == slot_folds[0], fold_of == slot_folds[1]]
    picked = jnp.minimum(jnp.stack(slot_folds), FOLDS - 1)

    gram_parts = []
    cross_parts = []
    for member in range(member_count):
        columns = jnp.pad(column_sets[member], ((0, 0), (0, padded_width - SNPS)))
        slot_grams = []
        slot_crosses = []
        for slot in range(2):
            masked = jnp.where(slot_masks[slot][:, None], columns, jnp.zeros_like(columns))
            slot_grams.append(tile_grams(masked, columns, panels))
            slot_crosses.append(inner_products(masked, ordered))
        gram_parts.append(jnp.stack(slot_grams))
        cross_parts.append(jnp.stack(slot_crosses))
    local_grams = jnp.stack(gram_parts, axis=1)
    local_crosses = jnp.stack(cross_parts, axis=1)

    wanted = []
    for device in range(devices):
        for offset in range(span):
            wanted.append(min(firsts[device] + offset, pair_count - 1))
    wanted_folds = jnp.array([pair // member_count for pair in wanted], jnp.int32)
    wanted_members = jnp.array([pair % member_count for pair in wanted], jnp.int32)
    member_axis = jnp.arange(member_count, dtype=jnp.int32)
    coefficient = jnp.stack(
        [
            jnp.logical_and(wanted_folds[:, None] != slot_folds[slot], wanted_members[:, None] == member_axis[None, :])
            for slot in range(2)
        ],
        axis=1,
    ).astype(jnp.float32)
    gram_payload = jnp.einsum("wjm,jmtab->wtab", coefficient, local_grams, precision=HIGH)
    cross_payload = jnp.einsum("wjm,jmic->wic", coefficient, local_crosses, precision=HIGH)
    gram_rows = gram_payload.reshape(devices, span * tile_count * PANEL, PANEL)
    cross_rows = cross_payload.reshape(devices, span * padded_width * traits // PANEL, PANEL)
    payload = jnp.concatenate([gram_rows, cross_rows], axis=1)
    reduced = lax.psum_scatter(payload, "sample", scatter_dimension=0, tiled=True)[0]
    split = span * tile_count * PANEL
    mine_grams = reduced[:split].reshape(span, tile_count, PANEL, PANEL)
    mine_crosses = reduced[split:].reshape(span, padded_width, traits)

    owned_ids = jnp.minimum(me * share + lax.broadcasted_iota(jnp.int32, (share,), 0), systems - 1)
    pair_ids = owned_ids // ridge_count
    ridge_ids = owned_ids % ridge_count
    local_ids = pair_ids - jnp.take(jnp.array(firsts, jnp.int32), me)
    rest_tiles = jnp.take(mine_grams, local_ids, axis=0)
    rest_crosses = jnp.take(mine_crosses, local_ids, axis=0)
    chosen_counts = jnp.take(counts, pair_ids // member_count, axis=0)
    ridge = jnp.take(shrinkage, ridge_ids, axis=0)
    diag_ids = [index for index, (row_tile, col_tile) in enumerate(tile_pairs(panels)) if row_tile == col_tile]
    is_diag = jnp.zeros((tile_count,), jnp.float32).at[jnp.array(diag_ids)].set(1.0)
    position = lax.broadcasted_iota(jnp.int32, (panels, PANEL), 1) + PANEL * lax.broadcasted_iota(
        jnp.int32, (panels, PANEL), 0
    )
    padded = (position >= SNPS).astype(jnp.float32)
    pad_diag = jnp.zeros((tile_count, PANEL), jnp.float32).at[jnp.array(diag_ids)].set(padded)
    identity = jnp.eye(PANEL, dtype=jnp.float32)
    diag_add = (
        ridge[:, None, None] * is_diag[None, :, None]
        + (1.0 - ridge[:, None, None]) * pad_diag[None, :, :]
    )
    system = rest_tiles / chosen_counts[:, None, None, None] + diag_add[:, :, :, None] * identity
    target = rest_crosses / chosen_counts[:, None, None]
    solved = block_solve(system, target, panels)[:, :SNPS].astype(jnp.bfloat16)
    collected = lax.all_gather(solved, "sample", axis=0, tiled=True)
    every_weights = collected[:systems].reshape(FOLDS, member_count, ridge_count, SNPS, traits)
    weights = jnp.take(every_weights, picked, axis=0)

    def fold_predictions(member, slot_weights):
        columns = column_sets[member]
        lower = predict(columns, slot_weights[0])
        upper = predict(columns, slot_weights[1])
        return jnp.where(slot_masks[1][None, None, :], upper, lower)

    local_preds = jnp.concatenate(
        [fold_predictions(member, weights[:, member]) for member in range(member_count)], axis=1
    )
    return lax.all_to_all(local_preds, "block", split_axis=0, concat_axis=1, tiled=True)


def solution(mesh):
    in_specs = (P("sample", "block"), P("block"), P("sample", None), P(), P())
    out_specs = P("block", None, "sample")
    return jax.shard_map(shards, mesh=mesh, in_specs=in_specs, out_specs=out_specs, check_vma=False)
```

```python
import jax
import jax.numpy as jnp
from jax import lax
from jax.experimental import pallas as pl
from jax.experimental.pallas import tpu as pltpu
from jax.sharding import PartitionSpec as P

SNPS = 500
FOLDS = 5
PANEL = 128
HIGH = lax.Precision.HIGHEST


def standardize(genotype, allele_freq):
    spread = jnp.sqrt(2.0 * allele_freq * (1.0 - allele_freq))
    return ((genotype.astype(jnp.float32) - 2.0 * allele_freq) / spread).astype(jnp.bfloat16)


def predict(columns, weights):
    stacked = jnp.transpose(weights, (2, 0, 1)).reshape(-1, weights.shape[1])
    product = lax.dot_general(
        stacked, columns, (((1,), (1,)), ((), ())), preferred_element_type=jnp.float32
    )
    return product.astype(jnp.bfloat16).reshape(
        weights.shape[2], weights.shape[0], columns.shape[0]
    )


def inner_products(left_cols, right_cols):
    return lax.dot_general(
        left_cols, right_cols, (((0,), (0,)), ((), ())), preferred_element_type=jnp.float32
    )


def tile_pairs(panels):
    pairs = []
    for row_tile in range(panels):
        for col_tile in range(row_tile, panels):
            pairs.append((row_tile, col_tile))
    return pairs


def tile_grams(left_cols, right_cols, panels):
    tile_list = []
    for row_tile, col_tile in tile_pairs(panels):
        first = left_cols[:, row_tile * PANEL : (row_tile + 1) * PANEL]
        second = right_cols[:, col_tile * PANEL : (col_tile + 1) * PANEL]
        tile_list.append(inner_products(first, second))
    return jnp.stack(tile_list)


def mm(spec, left, right):
    return jnp.einsum(spec, left, right, precision=HIGH, preferred_element_type=jnp.float32)


def inverse_factor_kernel(d_ref, w_ref, a_scr):
    count, n, _ = d_ref.shape
    a_scr[...] = d_ref[...]
    sub = lax.broadcasted_iota(jnp.int32, (n, n), 0)
    lane = lax.broadcasted_iota(jnp.int32, (n, n), 1)
    eye = jnp.where(sub == lane, 1.0, 0.0).astype(jnp.float32)
    for s in range(count):
        w_ref[s] = eye
    row_lane = lax.broadcasted_iota(jnp.int32, (1, n), 1)
    col_sub = lax.broadcasted_iota(jnp.int32, (n, 1), 0)

    def step(j, carry):
        for s in range(count):
            a = a_scr[s]
            row = jnp.sum(jnp.where(sub == j, a, 0.0), axis=0, keepdims=True)
            piv = jnp.sum(jnp.where(row_lane == j, row, 0.0), axis=1, keepdims=True)
            scale = 1.0 / jnp.sqrt(piv)
            col = jnp.sum(jnp.where(lane == j, a, 0.0), axis=1, keepdims=True)
            lcol = jnp.where(col_sub >= j, col * scale, 0.0)
            lrow = jnp.where(row_lane >= j, row * scale, 0.0)
            a_scr[s] = a - lcol * lrow
            r = w_ref[s]
            xrow = jnp.sum(jnp.where(sub == j, r, 0.0), axis=0, keepdims=True) * scale
            strict = jnp.where(col_sub > j, lcol, 0.0)
            w_ref[s] = jnp.where(sub == j, xrow, r - strict * xrow)
        return carry

    lax.fori_loop(0, n, step, 0)


def inverse_factor(block):
    count, n, _ = block.shape
    return pl.pallas_call(
        inverse_factor_kernel,
        out_shape=jax.ShapeDtypeStruct(block.shape, jnp.float32),
        in_specs=[pl.BlockSpec(memory_space=pltpu.VMEM)],
        out_specs=pl.BlockSpec(memory_space=pltpu.VMEM),
        scratch_shapes=[pltpu.VMEM(block.shape, jnp.float32)],
        cost_estimate=pl.CostEstimate(
            flops=12 * count * n * n * n, bytes_accessed=8 * count * n * n, transcendentals=count * n
        ),
    )(block)


def block_solve(tiles, target, panels):
    pairs = tile_pairs(panels)
    upper = {pair: tiles[:, index] for index, pair in enumerate(pairs)}
    lower = {}
    inverse = {}
    for p in range(panels):
        inv = inverse_factor(upper[(p, p)])
        inverse[p] = inv
        for q in range(p + 1, panels):
            lower[(q, p)] = mm("sji,skj->sik", upper[(p, q)], inv)
        for r in range(p + 1, panels):
            for q in range(r, panels):
                upper[(r, q)] = upper[(r, q)] - mm("sik,sjk->sij", lower[(r, p)], lower[(q, p)])
    forward = []
    for p in range(panels):
        rhs = target[:, p * PANEL : (p + 1) * PANEL]
        for q in range(p):
            rhs = rhs - mm("sij,sjc->sic", lower[(p, q)], forward[q])
        forward.append(mm("sij,sjc->sic", inverse[p], rhs))
    backward = [None] * panels
    for p in reversed(range(panels)):
        rhs = forward[p]
        for q in range(p + 1, panels):
            rhs = rhs - mm("sji,sjc->sic", lower[(q, p)], backward[q])
        backward[p] = mm("sji,sjc->sic", inverse[p], rhs)
    return jnp.concatenate(backward, axis=1)


def owned_layout(systems, devices, ridge_count):
    share = -(-systems // devices)
    firsts = []
    spans = []
    for device in range(devices):
        first = min(device * share, systems - 1) // ridge_count
        last = min(device * share + share - 1, systems - 1) // ridge_count
        firsts.append(first)
        spans.append(last - first + 1)
    return share, firsts, max(spans)


def shards(genotype, allele_freq, phenotype, shrinkage, owner_order):
    sample_rows = genotype.shape[0]
    devices = lax.axis_size("sample")
    me = lax.axis_index("sample")
    total_rows = sample_rows * devices
    scaled = standardize(genotype, allele_freq)
    ordered = jnp.take(phenotype, owner_order, axis=1)
    traits = ordered.shape[1]
    member_count = allele_freq.shape[0] // SNPS
    ridge_count = shrinkage.shape[0]
    panels = -(-SNPS // PANEL)
    padded_width = panels * PANEL
    tile_count = len(tile_pairs(panels))
    pair_count = FOLDS * member_count
    systems = pair_count * ridge_count
    share, firsts, span = owned_layout(systems, devices, ridge_count)
    column_sets = [scaled[:, member * SNPS : (member + 1) * SNPS] for member in range(member_count)]
    bounds = [-(-(k * total_rows) // FOLDS) for k in range(FOLDS + 1)]
    counts = jnp.array(
        [float(total_rows - (bounds[k + 1] - bounds[k])) for k in range(FOLDS)], dtype=jnp.float32
    )
    start_row = me * sample_rows
    row_ids = start_row + lax.broadcasted_iota(jnp.int32, (sample_rows,), 0)
    fold_of = row_ids * FOLDS // total_rows
    first_fold = start_row * FOLDS // total_rows
    slot_folds = [first_fold, first_fold + 1]
    slot_masks = [fold_of == slot_folds[0], fold_of == slot_folds[1]]
    picked = jnp.minimum(jnp.stack(slot_folds), FOLDS - 1)

    slot_rows = []
    for slot in range(2):
        member_rows = []
        for member in range(member_count):
            columns = jnp.pad(column_sets[member], ((0, 0), (0, padded_width - SNPS)))
            masked = jnp.where(slot_masks[slot][:, None], columns, jnp.zeros_like(columns))
            tiles = tile_grams(masked, columns, panels)
            cross = jnp.stack(
                [inner_products(ordered, masked[:, p * PANEL : (p + 1) * PANEL]) for p in range(panels)]
            )
            member_rows.append(jnp.concatenate([tiles.reshape(-1, PANEL), cross.reshape(-1, PANEL)]))
        slot_rows.append(jnp.stack(member_rows))
    local_rows = jnp.stack(slot_rows)

    wanted = []
    for device in range(devices):
        for offset in range(span):
            wanted.append(min(firsts[device] + offset, pair_count - 1))
    wanted_folds = jnp.array([pair // member_count for pair in wanted], jnp.int32)
    wanted_members = jnp.array([pair % member_count for pair in wanted], jnp.int32)
    member_axis = jnp.arange(member_count, dtype=jnp.int32)
    coefficient = jnp.stack(
        [
            jnp.logical_and(wanted_folds[:, None] != slot_folds[slot], wanted_members[:, None] == member_axis[None, :])
            for slot in range(2)
        ],
        axis=1,
    ).astype(jnp.float32)
    payload = jnp.sum(coefficient[:, :, :, None, None] * local_rows[None], axis=(1, 2))
    row_count = local_rows.shape[2]
    payload = payload.reshape(devices, span * row_count, PANEL)
    reduced = lax.psum_scatter(payload, "sample", scatter_dimension=0, tiled=True)[0]
    reduced = reduced.reshape(span, row_count, PANEL)
    split = tile_count * PANEL
    mine_grams = reduced[:, :split].reshape(span, tile_count, PANEL, PANEL)
    mine_crosses = reduced[:, split:].reshape(span, panels, traits, PANEL)

    owned_ids = jnp.minimum(me * share + lax.broadcasted_iota(jnp.int32, (share,), 0), systems - 1)
    pair_ids = owned_ids // ridge_count
    ridge_ids = owned_ids % ridge_count
    local_ids = pair_ids - jnp.take(jnp.array(firsts, jnp.int32), me)
    rest_tiles = jnp.take(mine_grams, local_ids, axis=0)
    rest_crosses = jnp.take(mine_crosses, local_ids, axis=0)
    chosen_counts = jnp.take(counts, pair_ids // member_count, axis=0)
    ridge = jnp.take(shrinkage, ridge_ids, axis=0)
    diag_ids = [index for index, (row_tile, col_tile) in enumerate(tile_pairs(panels)) if row_tile == col_tile]
    is_diag = jnp.zeros((tile_count,), jnp.float32).at[jnp.array(diag_ids)].set(1.0)
    position = lax.broadcasted_iota(jnp.int32, (panels, PANEL), 1) + PANEL * lax.broadcasted_iota(
        jnp.int32, (panels, PANEL), 0
    )
    padded = (position >= SNPS).astype(jnp.float32)
    pad_diag = jnp.zeros((tile_count, PANEL), jnp.float32).at[jnp.array(diag_ids)].set(padded)
    identity = jnp.eye(PANEL, dtype=jnp.float32)
    diag_add = (
        ridge[:, None, None] * is_diag[None, :, None]
        + (1.0 - ridge[:, None, None]) * pad_diag[None, :, :]
    )
    system = rest_tiles / chosen_counts[:, None, None, None] + diag_add[:, :, :, None] * identity
    target = jnp.swapaxes(rest_crosses, 2, 3).reshape(share, padded_width, traits)
    target = target / chosen_counts[:, None, None]
    solved = block_solve(system, target, panels)[:, :SNPS].astype(jnp.bfloat16)
    collected = lax.all_gather(solved, "sample", axis=0, tiled=True)
    every_weights = collected[:systems].reshape(FOLDS, member_count, ridge_count, SNPS, traits)
    weights = jnp.take(every_weights, picked, axis=0)

    def fold_predictions(member, slot_weights):
        columns = column_sets[member]
        lower = predict(columns, slot_weights[0])
        upper = predict(columns, slot_weights[1])
        return jnp.where(slot_masks[1][None, None, :], upper, lower)

    local_preds = jnp.concatenate(
        [fold_predictions(member, weights[:, member]) for member in range(member_count)], axis=1
    )
    return lax.all_to_all(local_preds, "block", split_axis=0, concat_axis=1, tiled=True)


def solution(mesh):
    in_specs = (P("sample", "block"), P("block"), P("sample", None), P(), P())
    out_specs = P("block", None, "sample")
    return jax.shard_map(shards, mesh=mesh, in_specs=in_specs, out_specs=out_specs, check_vma=False)
```

```python
import jax
import jax.numpy as jnp
from jax import lax
from jax.experimental import pallas as pl
from jax.experimental.pallas import tpu as pltpu
from jax.sharding import PartitionSpec as P

SNPS = 500
FOLDS = 5
PANEL = 128
HIGH = lax.Precision.HIGHEST


def standardize(genotype, allele_freq):
    spread = jnp.sqrt(2.0 * allele_freq * (1.0 - allele_freq))
    return ((genotype.astype(jnp.float32) - 2.0 * allele_freq) / spread).astype(jnp.bfloat16)


def predict(columns, weights):
    stacked = jnp.transpose(weights, (2, 0, 1)).reshape(-1, weights.shape[1])
    product = lax.dot_general(
        stacked, columns, (((1,), (1,)), ((), ())), preferred_element_type=jnp.float32
    )
    return product.astype(jnp.bfloat16).reshape(
        weights.shape[2], weights.shape[0], columns.shape[0]
    )


def inner_products(left_cols, right_cols):
    return lax.dot_general(
        left_cols, right_cols, (((0,), (0,)), ((), ())), preferred_element_type=jnp.float32
    )


def tile_pairs(panels):
    pairs = []
    for row_tile in range(panels):
        for col_tile in range(row_tile, panels):
            pairs.append((row_tile, col_tile))
    return pairs


def tile_grams(left_cols, right_cols, panels):
    tile_list = []
    for row_tile, col_tile in tile_pairs(panels):
        first = left_cols[:, row_tile * PANEL : (row_tile + 1) * PANEL]
        second = right_cols[:, col_tile * PANEL : (col_tile + 1) * PANEL]
        tile_list.append(inner_products(first, second))
    return jnp.stack(tile_list)


def mm(spec, left, right):
    return jnp.einsum(spec, left, right, precision=HIGH, preferred_element_type=jnp.float32)


def inverse_factor_kernel(d_ref, w_ref, a_scr):
    count, n, _ = d_ref.shape
    a_scr[...] = d_ref[...]
    sub = lax.broadcasted_iota(jnp.int32, (n, n), 0)
    lane = lax.broadcasted_iota(jnp.int32, (n, n), 1)
    eye = jnp.where(sub == lane, 1.0, 0.0).astype(jnp.float32)
    for s in range(count):
        w_ref[s] = eye
    row_lane = lax.broadcasted_iota(jnp.int32, (1, n), 1)
    col_sub = lax.broadcasted_iota(jnp.int32, (n, 1), 0)

    def step(j, carry):
        for s in range(count):
            a = a_scr[s]
            row = jnp.sum(jnp.where(sub == j, a, 0.0), axis=0, keepdims=True)
            piv = jnp.sum(jnp.where(row_lane == j, row, 0.0), axis=1, keepdims=True)
            scale = 1.0 / jnp.sqrt(piv)
            col = jnp.sum(jnp.where(lane == j, a, 0.0), axis=1, keepdims=True)
            lcol = jnp.where(col_sub >= j, col * scale, 0.0)
            lrow = jnp.where(row_lane >= j, row * scale, 0.0)
            a_scr[s] = a - lcol * lrow
            r = w_ref[s]
            xrow = jnp.sum(jnp.where(sub == j, r, 0.0), axis=0, keepdims=True) * scale
            strict = jnp.where(col_sub > j, lcol, 0.0)
            w_ref[s] = jnp.where(sub == j, xrow, r - strict * xrow)
        return carry

    lax.fori_loop(0, n, step, 0)


def inverse_factor(block):
    count, n, _ = block.shape
    return pl.pallas_call(
        inverse_factor_kernel,
        out_shape=jax.ShapeDtypeStruct(block.shape, jnp.float32),
        in_specs=[pl.BlockSpec(memory_space=pltpu.VMEM)],
        out_specs=pl.BlockSpec(memory_space=pltpu.VMEM),
        scratch_shapes=[pltpu.VMEM(block.shape, jnp.float32)],
        cost_estimate=pl.CostEstimate(
            flops=12 * count * n * n * n, bytes_accessed=8 * count * n * n, transcendentals=count * n
        ),
    )(block)


def block_solve(tiles, target, panels):
    pairs = tile_pairs(panels)
    upper = {pair: tiles[:, index] for index, pair in enumerate(pairs)}
    lower = {}
    inverse = {}
    for p in range(panels):
        inv = inverse_factor(upper[(p, p)])
        inverse[p] = inv
        for q in range(p + 1, panels):
            lower[(q, p)] = mm("sji,skj->sik", upper[(p, q)], inv)
        for r in range(p + 1, panels):
            for q in range(r, panels):
                upper[(r, q)] = upper[(r, q)] - mm("sik,sjk->sij", lower[(r, p)], lower[(q, p)])
    forward = []
    for p in range(panels):
        rhs = target[:, p * PANEL : (p + 1) * PANEL]
        for q in range(p):
            rhs = rhs - mm("sij,sjc->sic", lower[(p, q)], forward[q])
        forward.append(mm("sij,sjc->sic", inverse[p], rhs))
    backward = [None] * panels
    for p in reversed(range(panels)):
        rhs = forward[p]
        for q in range(p + 1, panels):
            rhs = rhs - mm("sji,sjc->sic", lower[(q, p)], backward[q])
        backward[p] = mm("sji,sjc->sic", inverse[p], rhs)
    return jnp.concatenate(backward, axis=1)


def owned_layout(systems, devices, ridge_count):
    share = -(-systems // devices)
    firsts = []
    spans = []
    for device in range(devices):
        first = min(device * share, systems - 1) // ridge_count
        last = min(device * share + share - 1, systems - 1) // ridge_count
        firsts.append(first)
        spans.append(last - first + 1)
    return share, firsts, max(spans)


def shards(genotype, allele_freq, phenotype, shrinkage, owner_order):
    sample_rows = genotype.shape[0]
    devices = lax.axis_size("sample")
    me = lax.axis_index("sample")
    total_rows = sample_rows * devices
    scaled = standardize(genotype, allele_freq)
    ordered = jnp.take(phenotype, owner_order, axis=1)
    traits = ordered.shape[1]
    member_count = allele_freq.shape[0] // SNPS
    ridge_count = shrinkage.shape[0]
    panels = -(-SNPS // PANEL)
    padded_width = panels * PANEL
    tile_count = len(tile_pairs(panels))
    pair_count = FOLDS * member_count
    systems = pair_count * ridge_count
    share, firsts, span = owned_layout(systems, devices, ridge_count)
    column_sets = [scaled[:, member * SNPS : (member + 1) * SNPS] for member in range(member_count)]
    bounds = [-(-(k * total_rows) // FOLDS) for k in range(FOLDS + 1)]
    counts = jnp.array(
        [float(total_rows - (bounds[k + 1] - bounds[k])) for k in range(FOLDS)], dtype=jnp.float32
    )
    start_row = me * sample_rows
    row_ids = start_row + lax.broadcasted_iota(jnp.int32, (sample_rows,), 0)
    fold_of = row_ids * FOLDS // total_rows
    first_fold = start_row * FOLDS // total_rows
    slot_folds = [first_fold, first_fold + 1]
    slot_masks = [fold_of == slot_folds[0], fold_of == slot_folds[1]]
    picked = jnp.minimum(jnp.stack(slot_folds), FOLDS - 1)

    slot_rows = []
    for slot in range(2):
        member_rows = []
        for member in range(member_count):
            columns = jnp.pad(column_sets[member], ((0, 0), (0, padded_width - SNPS)))
            masked = jnp.where(slot_masks[slot][:, None], columns, jnp.zeros_like(columns))
            tiles = tile_grams(masked, columns, panels)
            cross = jnp.stack(
                [inner_products(ordered, masked[:, p * PANEL : (p + 1) * PANEL]) for p in range(panels)]
            )
            member_rows.append(jnp.concatenate([tiles.reshape(-1, PANEL), cross.reshape(-1, PANEL)]))
        slot_rows.append(jnp.stack(member_rows))
    local_rows = jnp.stack(slot_rows)

    wanted = []
    for device in range(devices):
        for offset in range(span):
            wanted.append(min(firsts[device] + offset, pair_count - 1))
    wanted_folds = jnp.array([pair // member_count for pair in wanted], jnp.int32)
    wanted_members = jnp.array([pair % member_count for pair in wanted], jnp.int32)
    member_axis = jnp.arange(member_count, dtype=jnp.int32)
    coefficient = jnp.stack(
        [
            jnp.logical_and(wanted_folds[:, None] != slot_folds[slot], wanted_members[:, None] == member_axis[None, :])
            for slot in range(2)
        ],
        axis=1,
    ).astype(jnp.float32)
    payload = None
    for slot in range(2):
        for member in range(member_count):
            term = coefficient[:, slot, member][:, None, None] * local_rows[slot, member][None]
            payload = term if payload is None else payload + term
    row_count = local_rows.shape[2]
    payload = payload.reshape(devices, span * row_count, PANEL)
    reduced = lax.psum_scatter(payload, "sample", scatter_dimension=0, tiled=True)[0]
    reduced = reduced.reshape(span, row_count, PANEL)
    split = tile_count * PANEL
    mine_grams = reduced[:, :split].reshape(span, tile_count, PANEL, PANEL)
    mine_crosses = reduced[:, split:].reshape(span, panels, traits, PANEL)

    owned_ids = jnp.minimum(me * share + lax.broadcasted_iota(jnp.int32, (share,), 0), systems - 1)
    pair_ids = owned_ids // ridge_count
    ridge_ids = owned_ids % ridge_count
    local_ids = pair_ids - jnp.take(jnp.array(firsts, jnp.int32), me)
    rest_tiles = jnp.take(mine_grams, local_ids, axis=0)
    rest_crosses = jnp.take(mine_crosses, local_ids, axis=0)
    chosen_counts = jnp.take(counts, pair_ids // member_count, axis=0)
    ridge = jnp.take(shrinkage, ridge_ids, axis=0)
    diag_ids = [index for index, (row_tile, col_tile) in enumerate(tile_pairs(panels)) if row_tile == col_tile]
    is_diag = jnp.zeros((tile_count,), jnp.float32).at[jnp.array(diag_ids)].set(1.0)
    position = lax.broadcasted_iota(jnp.int32, (panels, PANEL), 1) + PANEL * lax.broadcasted_iota(
        jnp.int32, (panels, PANEL), 0
    )
    padded = (position >= SNPS).astype(jnp.float32)
    pad_diag = jnp.zeros((tile_count, PANEL), jnp.float32).at[jnp.array(diag_ids)].set(padded)
    identity = jnp.eye(PANEL, dtype=jnp.float32)
    diag_add = (
        ridge[:, None, None] * is_diag[None, :, None]
        + (1.0 - ridge[:, None, None]) * pad_diag[None, :, :]
    )
    system = rest_tiles / chosen_counts[:, None, None, None] + diag_add[:, :, :, None] * identity
    target = jnp.swapaxes(rest_crosses, 2, 3).reshape(share, padded_width, traits)
    target = target / chosen_counts[:, None, None]
    solved = block_solve(system, target, panels)[:, :SNPS].astype(jnp.bfloat16)
    collected = lax.all_gather(solved, "sample", axis=0, tiled=True)
    every_weights = collected[:systems].reshape(FOLDS, member_count, ridge_count, SNPS, traits)
    weights = jnp.take(every_weights, picked, axis=0)

    def fold_predictions(member, slot_weights):
        columns = column_sets[member]
        lower = predict(columns, slot_weights[0])
        upper = predict(columns, slot_weights[1])
        return jnp.where(slot_masks[1][None, None, :], upper, lower)

    local_preds = jnp.concatenate(
        [fold_predictions(member, weights[:, member]) for member in range(member_count)], axis=1
    )
    return lax.all_to_all(local_preds, "block", split_axis=0, concat_axis=1, tiled=True)


def solution(mesh):
    in_specs = (P("sample", "block"), P("block"), P("sample", None), P(), P())
    out_specs = P("block", None, "sample")
    return jax.shard_map(shards, mesh=mesh, in_specs=in_specs, out_specs=out_specs, check_vma=False)
```

```python
import jax
import jax.numpy as jnp
from jax import lax
from jax.experimental import pallas as pl
from jax.experimental.pallas import tpu as pltpu
from jax.sharding import PartitionSpec as P

SNPS = 500
FOLDS = 5
PANEL = 128
HIGH = lax.Precision.HIGHEST


def standardize(genotype, allele_freq):
    spread = jnp.sqrt(2.0 * allele_freq * (1.0 - allele_freq))
    return ((genotype.astype(jnp.float32) - 2.0 * allele_freq) / spread).astype(jnp.bfloat16)


def predict(columns, weights):
    stacked = jnp.transpose(weights, (2, 0, 1)).reshape(-1, weights.shape[1])
    product = lax.dot_general(
        stacked, columns, (((1,), (1,)), ((), ())), preferred_element_type=jnp.float32
    )
    return product.astype(jnp.bfloat16).reshape(
        weights.shape[2], weights.shape[0], columns.shape[0]
    )


def inner_products(left_cols, right_cols):
    return lax.dot_general(
        left_cols, right_cols, (((0,), (0,)), ((), ())), preferred_element_type=jnp.float32
    )


def tile_pairs(panels):
    pairs = []
    for row_tile in range(panels):
        for col_tile in range(row_tile, panels):
            pairs.append((row_tile, col_tile))
    return pairs


def tile_grams(left_cols, right_cols, panels):
    tile_list = []
    for row_tile, col_tile in tile_pairs(panels):
        first = left_cols[:, row_tile * PANEL : (row_tile + 1) * PANEL]
        second = right_cols[:, col_tile * PANEL : (col_tile + 1) * PANEL]
        tile_list.append(inner_products(first, second))
    return jnp.stack(tile_list)


def mm(spec, left, right):
    return jnp.einsum(spec, left, right, precision=HIGH, preferred_element_type=jnp.float32)


def inverse_factor_kernel(d_ref, w_ref, a_scr):
    count, n, _ = d_ref.shape
    a_scr[...] = d_ref[...]
    sub = lax.broadcasted_iota(jnp.int32, (n, n), 0)
    lane = lax.broadcasted_iota(jnp.int32, (n, n), 1)
    eye = jnp.where(sub == lane, 1.0, 0.0).astype(jnp.float32)
    for s in range(count):
        w_ref[s] = eye
    row_lane = lax.broadcasted_iota(jnp.int32, (1, n), 1)
    col_sub = lax.broadcasted_iota(jnp.int32, (n, 1), 0)

    def step(j, carry):
        for s in range(count):
            a = a_scr[s]
            row = jnp.sum(jnp.where(sub == j, a, 0.0), axis=0, keepdims=True)
            piv = jnp.sum(jnp.where(row_lane == j, row, 0.0), axis=1, keepdims=True)
            scale = 1.0 / jnp.sqrt(piv)
            col = jnp.sum(jnp.where(lane == j, a, 0.0), axis=1, keepdims=True)
            lcol = jnp.where(col_sub >= j, col * scale, 0.0)
            lrow = jnp.where(row_lane >= j, row * scale, 0.0)
            a_scr[s] = a - lcol * lrow
            r = w_ref[s]
            xrow = jnp.sum(jnp.where(sub == j, r, 0.0), axis=0, keepdims=True) * scale
            strict = jnp.where(col_sub > j, lcol, 0.0)
            w_ref[s] = jnp.where(sub == j, xrow, r - strict * xrow)
        return carry

    lax.fori_loop(0, n, step, 0)


def inverse_factor(block):
    count, n, _ = block.shape
    return pl.pallas_call(
        inverse_factor_kernel,
        out_shape=jax.ShapeDtypeStruct(block.shape, jnp.float32),
        in_specs=[pl.BlockSpec(memory_space=pltpu.VMEM)],
        out_specs=pl.BlockSpec(memory_space=pltpu.VMEM),
        scratch_shapes=[pltpu.VMEM(block.shape, jnp.float32)],
        cost_estimate=pl.CostEstimate(
            flops=12 * count * n * n * n, bytes_accessed=8 * count * n * n, transcendentals=count * n
        ),
    )(block)


def block_solve(tiles, target, panels):
    pairs = tile_pairs(panels)
    bands = []
    for row_tile in range(panels):
        band = []
        for col_tile in range(panels):
            if row_tile <= col_tile:
                band.append(tiles[:, pairs.index((row_tile, col_tile))])
            else:
                band.append(jnp.swapaxes(tiles[:, pairs.index((col_tile, row_tile))], 1, 2))
        bands.append(jnp.concatenate(band, axis=2))
    trailing = jnp.concatenate(bands, axis=1)
    inverses = []
    strips = []
    for p in range(panels):
        inv = inverse_factor(trailing[:, :PANEL, :PANEL])
        inverses.append(inv)
        if p + 1 < panels:
            strip = mm("sij,skj->sik", trailing[:, PANEL:, :PANEL], inv)
            strips.append(strip)
            trailing = trailing[:, PANEL:, PANEL:] - mm("sik,sjk->sij", strip, strip)
    residual = target
    forward = []
    for p in range(panels):
        y = mm("sij,sjc->sic", inverses[p], residual[:, :PANEL])
        forward.append(y)
        if p + 1 < panels:
            residual = residual[:, PANEL:] - mm("sij,sjc->sic", strips[p], y)
    solved = mm("sji,sjc->sic", inverses[panels - 1], forward[panels - 1])
    for p in reversed(range(panels - 1)):
        rhs = forward[p] - mm("sji,sjc->sic", strips[p], solved)
        solved = jnp.concatenate([mm("sji,sjc->sic", inverses[p], rhs), solved], axis=1)
    return solved


def owned_layout(systems, devices, ridge_count):
    share = -(-systems // devices)
    firsts = []
    spans = []
    for device in range(devices):
        first = min(device * share, systems - 1) // ridge_count
        last = min(device * share + share - 1, systems - 1) // ridge_count
        firsts.append(first)
        spans.append(last - first + 1)
    return share, firsts, max(spans)


def shards(genotype, allele_freq, phenotype, shrinkage, owner_order):
    sample_rows = genotype.shape[0]
    devices = lax.axis_size("sample")
    me = lax.axis_index("sample")
    total_rows = sample_rows * devices
    scaled = standardize(genotype, allele_freq)
    ordered = jnp.take(phenotype, owner_order, axis=1)
    traits = ordered.shape[1]
    member_count = allele_freq.shape[0] // SNPS
    ridge_count = shrinkage.shape[0]
    panels = -(-SNPS // PANEL)
    padded_width = panels * PANEL
    tile_count = len(tile_pairs(panels))
    pair_count = FOLDS * member_count
    systems = pair_count * ridge_count
    share, firsts, span = owned_layout(systems, devices, ridge_count)
    column_sets = [scaled[:, member * SNPS : (member + 1) * SNPS] for member in range(member_count)]
    bounds = [-(-(k * total_rows) // FOLDS) for k in range(FOLDS + 1)]
    counts = jnp.array(
        [float(total_rows - (bounds[k + 1] - bounds[k])) for k in range(FOLDS)], dtype=jnp.float32
    )
    start_row = me * sample_rows
    row_ids = start_row + lax.broadcasted_iota(jnp.int32, (sample_rows,), 0)
    fold_of = row_ids * FOLDS // total_rows
    first_fold = start_row * FOLDS // total_rows
    slot_folds = [first_fold, first_fold + 1]
    slot_masks = [fold_of == slot_folds[0], fold_of == slot_folds[1]]
    picked = jnp.minimum(jnp.stack(slot_folds), FOLDS - 1)

    slot_rows = []
    for slot in range(2):
        member_rows = []
        for member in range(member_count):
            columns = jnp.pad(column_sets[member], ((0, 0), (0, padded_width - SNPS)))
            masked = jnp.where(slot_masks[slot][:, None], columns, jnp.zeros_like(columns))
            tiles = tile_grams(masked, columns, panels)
            cross = jnp.stack(
                [inner_products(ordered, masked[:, p * PANEL : (p + 1) * PANEL]) for p in range(panels)]
            )
            member_rows.append(jnp.concatenate([tiles.reshape(-1, PANEL), cross.reshape(-1, PANEL)]))
        slot_rows.append(jnp.stack(member_rows))
    local_rows = jnp.stack(slot_rows)

    wanted = []
    for device in range(devices):
        for offset in range(span):
            wanted.append(min(firsts[device] + offset, pair_count - 1))
    wanted_folds = jnp.array([pair // member_count for pair in wanted], jnp.int32)
    wanted_members = jnp.array([pair % member_count for pair in wanted], jnp.int32)
    member_axis = jnp.arange(member_count, dtype=jnp.int32)
    coefficient = jnp.stack(
        [
            jnp.logical_and(wanted_folds[:, None] != slot_folds[slot], wanted_members[:, None] == member_axis[None, :])
            for slot in range(2)
        ],
        axis=1,
    ).astype(jnp.float32)
    payload = None
    for slot in range(2):
        for member in range(member_count):
            term = coefficient[:, slot, member][:, None, None] * local_rows[slot, member][None]
            payload = term if payload is None else payload + term
    row_count = local_rows.shape[2]
    payload = payload.reshape(devices, span * row_count, PANEL)
    reduced = lax.psum_scatter(payload, "sample", scatter_dimension=0, tiled=True)[0]
    reduced = reduced.reshape(span, row_count, PANEL)
    split = tile_count * PANEL
    mine_grams = reduced[:, :split].reshape(span, tile_count, PANEL, PANEL)
    mine_crosses = reduced[:, split:].reshape(span, panels, traits, PANEL)

    owned_ids = jnp.minimum(me * share + lax.broadcasted_iota(jnp.int32, (share,), 0), systems - 1)
    pair_ids = owned_ids // ridge_count
    ridge_ids = owned_ids % ridge_count
    local_ids = pair_ids - jnp.take(jnp.array(firsts, jnp.int32), me)
    rest_tiles = jnp.take(mine_grams, local_ids, axis=0)
    rest_crosses = jnp.take(mine_crosses, local_ids, axis=0)
    chosen_counts = jnp.take(counts, pair_ids // member_count, axis=0)
    ridge = jnp.take(shrinkage, ridge_ids, axis=0)
    diag_ids = [index for index, (row_tile, col_tile) in enumerate(tile_pairs(panels)) if row_tile == col_tile]
    is_diag = jnp.zeros((tile_count,), jnp.float32).at[jnp.array(diag_ids)].set(1.0)
    position = lax.broadcasted_iota(jnp.int32, (panels, PANEL), 1) + PANEL * lax.broadcasted_iota(
        jnp.int32, (panels, PANEL), 0
    )
    padded = (position >= SNPS).astype(jnp.float32)
    pad_diag = jnp.zeros((tile_count, PANEL), jnp.float32).at[jnp.array(diag_ids)].set(padded)
    identity = jnp.eye(PANEL, dtype=jnp.float32)
    diag_add = (
        ridge[:, None, None] * is_diag[None, :, None]
        + (1.0 - ridge[:, None, None]) * pad_diag[None, :, :]
    )
    system = rest_tiles / chosen_counts[:, None, None, None] + diag_add[:, :, :, None] * identity
    target = jnp.swapaxes(rest_crosses, 2, 3).reshape(share, padded_width, traits)
    target = target / chosen_counts[:, None, None]
    solved = block_solve(system, target, panels)[:, :SNPS].astype(jnp.bfloat16)
    collected = lax.all_gather(solved, "sample", axis=0, tiled=True)
    every_weights = collected[:systems].reshape(FOLDS, member_count, ridge_count, SNPS, traits)
    weights = jnp.take(every_weights, picked, axis=0)

    def fold_predictions(member, slot_weights):
        columns = column_sets[member]
        lower = predict(columns, slot_weights[0])
        upper = predict(columns, slot_weights[1])
        return jnp.where(slot_masks[1][None, None, :], upper, lower)

    local_preds = jnp.concatenate(
        [fold_predictions(member, weights[:, member]) for member in range(member_count)], axis=1
    )
    return lax.all_to_all(local_preds, "block", split_axis=0, concat_axis=1, tiled=True)


def solution(mesh):
    in_specs = (P("sample", "block"), P("block"), P("sample", None), P(), P())
    out_specs = P("block", None, "sample")
    return jax.shard_map(shards, mesh=mesh, in_specs=in_specs, out_specs=out_specs, check_vma=False)
```

```python
import jax
import jax.numpy as jnp
from jax import lax
from jax.experimental import pallas as pl
from jax.experimental.pallas import tpu as pltpu
from jax.sharding import PartitionSpec as P

SNPS = 500
FOLDS = 5
PANEL = 128
HIGH = lax.Precision.HIGHEST


def standardize(genotype, allele_freq):
    spread = jnp.sqrt(2.0 * allele_freq * (1.0 - allele_freq))
    return ((genotype.astype(jnp.float32) - 2.0 * allele_freq) / spread).astype(jnp.bfloat16)


def predict(columns, weights):
    stacked = jnp.transpose(weights, (2, 0, 1)).reshape(-1, weights.shape[1])
    product = lax.dot_general(
        stacked, columns, (((1,), (1,)), ((), ())), preferred_element_type=jnp.float32
    )
    return product.astype(jnp.bfloat16).reshape(
        weights.shape[2], weights.shape[0], columns.shape[0]
    )


def inner_products(left_cols, right_cols):
    return lax.dot_general(
        left_cols, right_cols, (((0,), (0,)), ((), ())), preferred_element_type=jnp.float32
    )


def tile_pairs(panels):
    pairs = []
    for row_tile in range(panels):
        for col_tile in range(row_tile, panels):
            pairs.append((row_tile, col_tile))
    return pairs


def tile_grams(left_cols, right_cols, panels):
    tile_list = []
    for row_tile, col_tile in tile_pairs(panels):
        first = left_cols[:, row_tile * PANEL : (row_tile + 1) * PANEL]
        second = right_cols[:, col_tile * PANEL : (col_tile + 1) * PANEL]
        tile_list.append(inner_products(first, second))
    return jnp.stack(tile_list)


def mm(spec, left, right):
    return jnp.einsum(spec, left, right, precision=HIGH, preferred_element_type=jnp.float32)


def inverse_factor_kernel(d_ref, w_ref, a_scr):
    count, n, _ = d_ref.shape
    a_scr[...] = d_ref[...]
    sub = lax.broadcasted_iota(jnp.int32, (n, n), 0)
    lane = lax.broadcasted_iota(jnp.int32, (n, n), 1)
    eye = jnp.where(sub == lane, 1.0, 0.0).astype(jnp.float32)
    for s in range(count):
        w_ref[s] = eye
    row_lane = lax.broadcasted_iota(jnp.int32, (1, n), 1)
    col_sub = lax.broadcasted_iota(jnp.int32, (n, 1), 0)

    def pick(row, k):
        return jnp.sum(jnp.where(row_lane == k, row, 0.0), axis=1, keepdims=True)

    def step(t, carry):
        j = 2 * t
        for s in range(count):
            a = a_scr[s]
            row0 = jnp.sum(jnp.where(sub == j, a, 0.0), axis=0, keepdims=True)
            row1 = jnp.sum(jnp.where(sub == j + 1, a, 0.0), axis=0, keepdims=True)
            col0 = jnp.sum(jnp.where(lane == j, a, 0.0), axis=1, keepdims=True)
            col1 = jnp.sum(jnp.where(lane == j + 1, a, 0.0), axis=1, keepdims=True)
            top = jnp.sqrt(pick(row0, j))
            inv_top = 1.0 / top
            off = pick(row0, j + 1) * inv_top
            bottom = jnp.sqrt(pick(row1, j + 1) - off * off)
            inv_bottom = 1.0 / bottom
            lcol0 = jnp.where(col_sub >= j, col0 * inv_top, 0.0)
            lrow0 = jnp.where(row_lane >= j, row0 * inv_top, 0.0)
            lcol1 = jnp.where(col_sub >= j + 1, (col1 - lcol0 * off) * inv_bottom, 0.0)
            lrow1 = jnp.where(row_lane >= j + 1, (row1 - lrow0 * off) * inv_bottom, 0.0)
            a_scr[s] = a - lcol0 * lrow0 - lcol1 * lrow1
            r = w_ref[s]
            x0 = jnp.sum(jnp.where(sub == j, r, 0.0), axis=0, keepdims=True) * inv_top
            w1 = jnp.sum(jnp.where(sub == j + 1, r, 0.0), axis=0, keepdims=True)
            x1 = (w1 - off * x0) * inv_bottom
            strict0 = jnp.where(col_sub > j + 1, lcol0, 0.0)
            strict1 = jnp.where(col_sub > j + 1, lcol1, 0.0)
            updated = r - strict0 * x0 - strict1 * x1
            w_ref[s] = jnp.where(sub == j, x0, jnp.where(sub == j + 1, x1, updated))
        return carry

    lax.fori_loop(0, n // 2, step, 0)


def inverse_factor(block):
    count, n, _ = block.shape
    return pl.pallas_call(
        inverse_factor_kernel,
        out_shape=jax.ShapeDtypeStruct(block.shape, jnp.float32),
        in_specs=[pl.BlockSpec(memory_space=pltpu.VMEM)],
        out_specs=pl.BlockSpec(memory_space=pltpu.VMEM),
        scratch_shapes=[pltpu.VMEM(block.shape, jnp.float32)],
        cost_estimate=pl.CostEstimate(
            flops=12 * count * n * n * n, bytes_accessed=8 * count * n * n, transcendentals=count * n
        ),
    )(block)


def block_solve(tiles, target, panels):
    pairs = tile_pairs(panels)
    bands = []
    for row_tile in range(panels):
        band = []
        for col_tile in range(panels):
            if row_tile <= col_tile:
                band.append(tiles[:, pairs.index((row_tile, col_tile))])
            else:
                band.append(jnp.swapaxes(tiles[:, pairs.index((col_tile, row_tile))], 1, 2))
        bands.append(jnp.concatenate(band, axis=2))
    trailing = jnp.concatenate(bands, axis=1)
    inverses = []
    strips = []
    for p in range(panels):
        inv = inverse_factor(trailing[:, :PANEL, :PANEL])
        inverses.append(inv)
        if p + 1 < panels:
            strip = mm("sij,skj->sik", trailing[:, PANEL:, :PANEL], inv)
            strips.append(strip)
            trailing = trailing[:, PANEL:, PANEL:] - mm("sik,sjk->sij", strip, strip)
    residual = target
    forward = []
    for p in range(panels):
        y = mm("sij,sjc->sic", inverses[p], residual[:, :PANEL])
        forward.append(y)
        if p + 1 < panels:
            residual = residual[:, PANEL:] - mm("sij,sjc->sic", strips[p], y)
    solved = mm("sji,sjc->sic", inverses[panels - 1], forward[panels - 1])
    for p in reversed(range(panels - 1)):
        rhs = forward[p] - mm("sji,sjc->sic", strips[p], solved)
        solved = jnp.concatenate([mm("sji,sjc->sic", inverses[p], rhs), solved], axis=1)
    return solved


def owned_layout(systems, devices, ridge_count):
    share = -(-systems // devices)
    firsts = []
    spans = []
    for device in range(devices):
        first = min(device * share, systems - 1) // ridge_count
        last = min(device * share + share - 1, systems - 1) // ridge_count
        firsts.append(first)
        spans.append(last - first + 1)
    return share, firsts, max(spans)


def shards(genotype, allele_freq, phenotype, shrinkage, owner_order):
    sample_rows = genotype.shape[0]
    devices = lax.axis_size("sample")
    me = lax.axis_index("sample")
    total_rows = sample_rows * devices
    scaled = standardize(genotype, allele_freq)
    ordered = jnp.take(phenotype, owner_order, axis=1)
    traits = ordered.shape[1]
    member_count = allele_freq.shape[0] // SNPS
    ridge_count = shrinkage.shape[0]
    panels = -(-SNPS // PANEL)
    padded_width = panels * PANEL
    tile_count = len(tile_pairs(panels))
    pair_count = FOLDS * member_count
    systems = pair_count * ridge_count
    share, firsts, span = owned_layout(systems, devices, ridge_count)
    column_sets = [scaled[:, member * SNPS : (member + 1) * SNPS] for member in range(member_count)]
    bounds = [-(-(k * total_rows) // FOLDS) for k in range(FOLDS + 1)]
    counts = jnp.array(
        [float(total_rows - (bounds[k + 1] - bounds[k])) for k in range(FOLDS)], dtype=jnp.float32
    )
    start_row = me * sample_rows
    row_ids = start_row + lax.broadcasted_iota(jnp.int32, (sample_rows,), 0)
    fold_of = row_ids * FOLDS // total_rows
    first_fold = start_row * FOLDS // total_rows
    slot_folds = [first_fold, first_fold + 1]
    slot_masks = [fold_of == slot_folds[0], fold_of == slot_folds[1]]
    picked = jnp.minimum(jnp.stack(slot_folds), FOLDS - 1)

    slot_rows = []
    for slot in range(2):
        member_rows = []
        for member in range(member_count):
            columns = jnp.pad(column_sets[member], ((0, 0), (0, padded_width - SNPS)))
            masked = jnp.where(slot_masks[slot][:, None], columns, jnp.zeros_like(columns))
            tiles = tile_grams(masked, columns, panels)
            cross = jnp.stack(
                [inner_products(ordered, masked[:, p * PANEL : (p + 1) * PANEL]) for p in range(panels)]
            )
            member_rows.append(jnp.concatenate([tiles.reshape(-1, PANEL), cross.reshape(-1, PANEL)]))
        slot_rows.append(jnp.stack(member_rows))
    local_rows = jnp.stack(slot_rows)

    wanted = []
    for device in range(devices):
        for offset in range(span):
            wanted.append(min(firsts[device] + offset, pair_count - 1))
    wanted_folds = jnp.array([pair // member_count for pair in wanted], jnp.int32)
    wanted_members = jnp.array([pair % member_count for pair in wanted], jnp.int32)
    member_axis = jnp.arange(member_count, dtype=jnp.int32)
    coefficient = jnp.stack(
        [
            jnp.logical_and(wanted_folds[:, None] != slot_folds[slot], wanted_members[:, None] == member_axis[None, :])
            for slot in range(2)
        ],
        axis=1,
    ).astype(jnp.float32)
    payload = None
    for slot in range(2):
        for member in range(member_count):
            term = coefficient[:, slot, member][:, None, None] * local_rows[slot, member][None]
            payload = term if payload is None else payload + term
    row_count = local_rows.shape[2]
    payload = payload.reshape(devices, span * row_count, PANEL)
    reduced = lax.psum_scatter(payload, "sample", scatter_dimension=0, tiled=True)[0]
    reduced = reduced.reshape(span, row_count, PANEL)
    split = tile_count * PANEL
    mine_grams = reduced[:, :split].reshape(span, tile_count, PANEL, PANEL)
    mine_crosses = reduced[:, split:].reshape(span, panels, traits, PANEL)

    owned_ids = jnp.minimum(me * share + lax.broadcasted_iota(jnp.int32, (share,), 0), systems - 1)
    pair_ids = owned_ids // ridge_count
    ridge_ids = owned_ids % ridge_count
    local_ids = pair_ids - jnp.take(jnp.array(firsts, jnp.int32), me)
    rest_tiles = jnp.take(mine_grams, local_ids, axis=0)
    rest_crosses = jnp.take(mine_crosses, local_ids, axis=0)
    chosen_counts = jnp.take(counts, pair_ids // member_count, axis=0)
    ridge = jnp.take(shrinkage, ridge_ids, axis=0)
    diag_ids = [index for index, (row_tile, col_tile) in enumerate(tile_pairs(panels)) if row_tile == col_tile]
    is_diag = jnp.zeros((tile_count,), jnp.float32).at[jnp.array(diag_ids)].set(1.0)
    position = lax.broadcasted_iota(jnp.int32, (panels, PANEL), 1) + PANEL * lax.broadcasted_iota(
        jnp.int32, (panels, PANEL), 0
    )
    padded = (position >= SNPS).astype(jnp.float32)
    pad_diag = jnp.zeros((tile_count, PANEL), jnp.float32).at[jnp.array(diag_ids)].set(padded)
    identity = jnp.eye(PANEL, dtype=jnp.float32)
    diag_add = (
        ridge[:, None, None] * is_diag[None, :, None]
        + (1.0 - ridge[:, None, None]) * pad_diag[None, :, :]
    )
    system = rest_tiles / chosen_counts[:, None, None, None] + diag_add[:, :, :, None] * identity
    target = jnp.swapaxes(rest_crosses, 2, 3).reshape(share, padded_width, traits)
    target = target / chosen_counts[:, None, None]
    solved = block_solve(system, target, panels)[:, :SNPS].astype(jnp.bfloat16)
    collected = lax.all_gather(solved, "sample", axis=0, tiled=True)
    every_weights = collected[:systems].reshape(FOLDS, member_count, ridge_count, SNPS, traits)
    weights = jnp.take(every_weights, picked, axis=0)

    def fold_predictions(member, slot_weights):
        columns = column_sets[member]
        lower = predict(columns, slot_weights[0])
        upper = predict(columns, slot_weights[1])
        return jnp.where(slot_masks[1][None, None, :], upper, lower)

    local_preds = jnp.concatenate(
        [fold_predictions(member, weights[:, member]) for member in range(member_count)], axis=1
    )
    return lax.all_to_all(local_preds, "block", split_axis=0, concat_axis=1, tiled=True)


def solution(mesh):
    in_specs = (P("sample", "block"), P("block"), P("sample", None), P(), P())
    out_specs = P("block", None, "sample")
    return jax.shard_map(shards, mesh=mesh, in_specs=in_specs, out_specs=out_specs, check_vma=False)
```

```python
import jax
import jax.numpy as jnp
from jax import lax
from jax.experimental import pallas as pl
from jax.experimental.pallas import tpu as pltpu
from jax.sharding import PartitionSpec as P

SNPS = 500
FOLDS = 5
PANEL = 128
HIGH = lax.Precision.HIGHEST


def standardize(genotype, allele_freq):
    spread = jnp.sqrt(2.0 * allele_freq * (1.0 - allele_freq))
    return ((genotype.astype(jnp.float32) - 2.0 * allele_freq) / spread).astype(jnp.bfloat16)


def predict(columns, weights):
    stacked = jnp.transpose(weights, (2, 0, 1)).reshape(-1, weights.shape[1])
    product = lax.dot_general(
        stacked, columns, (((1,), (1,)), ((), ())), preferred_element_type=jnp.float32
    )
    return product.astype(jnp.bfloat16).reshape(
        weights.shape[2], weights.shape[0], columns.shape[0]
    )


def inner_products(left_cols, right_cols):
    return lax.dot_general(
        left_cols, right_cols, (((0,), (0,)), ((), ())), preferred_element_type=jnp.float32
    )


def tile_pairs(panels):
    pairs = []
    for row_tile in range(panels):
        for col_tile in range(row_tile, panels):
            pairs.append((row_tile, col_tile))
    return pairs


def tile_grams(left_cols, right_cols, panels):
    tile_list = []
    for row_tile, col_tile in tile_pairs(panels):
        first = left_cols[:, row_tile * PANEL : (row_tile + 1) * PANEL]
        second = right_cols[:, col_tile * PANEL : (col_tile + 1) * PANEL]
        tile_list.append(inner_products(first, second))
    return jnp.stack(tile_list)


def mm(spec, left, right):
    return jnp.einsum(spec, left, right, precision=HIGH, preferred_element_type=jnp.float32)


def inverse_factor_kernel(d_ref, w_ref, a_scr):
    count, n, _ = d_ref.shape
    a_scr[...] = d_ref[...]
    sub = lax.broadcasted_iota(jnp.int32, (n, n), 0)
    lane = lax.broadcasted_iota(jnp.int32, (n, n), 1)
    eye = jnp.where(sub == lane, 1.0, 0.0).astype(jnp.float32)
    for s in range(count):
        w_ref[s] = eye
    row_lane = lax.broadcasted_iota(jnp.int32, (1, n), 1)
    col_sub = lax.broadcasted_iota(jnp.int32, (n, 1), 0)

    def pick(row, k):
        return jnp.sum(jnp.where(row_lane == k, row, 0.0), axis=1, keepdims=True)

    def step(t, carry):
        j = 2 * t
        for s in range(count):
            a = a_scr[s]
            row0 = jnp.sum(jnp.where(sub == j, a, 0.0), axis=0, keepdims=True)
            row1 = jnp.sum(jnp.where(sub == j + 1, a, 0.0), axis=0, keepdims=True)
            col0 = jnp.sum(jnp.where(lane == j, a, 0.0), axis=1, keepdims=True)
            col1 = jnp.sum(jnp.where(lane == j + 1, a, 0.0), axis=1, keepdims=True)
            top = jnp.sqrt(pick(row0, j))
            inv_top = 1.0 / top
            off = pick(row0, j + 1) * inv_top
            bottom = jnp.sqrt(pick(row1, j + 1) - off * off)
            inv_bottom = 1.0 / bottom
            lcol0 = jnp.where(col_sub >= j, col0 * inv_top, 0.0)
            lrow0 = jnp.where(row_lane >= j, row0 * inv_top, 0.0)
            lcol1 = jnp.where(col_sub >= j + 1, (col1 - lcol0 * off) * inv_bottom, 0.0)
            lrow1 = jnp.where(row_lane >= j + 1, (row1 - lrow0 * off) * inv_bottom, 0.0)
            a_scr[s] = a - lcol0 * lrow0 - lcol1 * lrow1
            r = w_ref[s]
            x0 = jnp.sum(jnp.where(sub == j, r, 0.0), axis=0, keepdims=True) * inv_top
            w1 = jnp.sum(jnp.where(sub == j + 1, r, 0.0), axis=0, keepdims=True)
            x1 = (w1 - off * x0) * inv_bottom
            strict0 = jnp.where(col_sub > j + 1, lcol0, 0.0)
            strict1 = jnp.where(col_sub > j + 1, lcol1, 0.0)
            updated = r - strict0 * x0 - strict1 * x1
            w_ref[s] = jnp.where(sub == j, x0, jnp.where(sub == j + 1, x1, updated))
        return carry

    lax.fori_loop(0, n // 2, step, 0)


def inverse_factor(block):
    count, n, _ = block.shape
    return pl.pallas_call(
        inverse_factor_kernel,
        out_shape=jax.ShapeDtypeStruct(block.shape, jnp.float32),
        in_specs=[pl.BlockSpec(memory_space=pltpu.VMEM)],
        out_specs=pl.BlockSpec(memory_space=pltpu.VMEM),
        scratch_shapes=[pltpu.VMEM(block.shape, jnp.float32)],
        cost_estimate=pl.CostEstimate(
            flops=12 * count * n * n * n, bytes_accessed=8 * count * n * n, transcendentals=count * n
        ),
    )(block)


def block_solve(tiles, target, panels):
    pairs = tile_pairs(panels)
    bands = []
    for row_tile in range(panels):
        band = []
        for col_tile in range(panels):
            if row_tile <= col_tile:
                band.append(tiles[:, pairs.index((row_tile, col_tile))])
            else:
                band.append(jnp.swapaxes(tiles[:, pairs.index((col_tile, row_tile))], 1, 2))
        bands.append(jnp.concatenate(band, axis=2))
    trailing = jnp.concatenate(bands, axis=1)
    inverses = []
    strips = []
    for p in range(panels):
        inv = inverse_factor(trailing[:, :PANEL, :PANEL])
        inverses.append(inv)
        if p + 1 < panels:
            strip = mm("sij,skj->sik", trailing[:, PANEL:, :PANEL], inv)
            strips.append(strip)
            trailing = trailing[:, PANEL:, PANEL:] - mm("sik,sjk->sij", strip, strip)
    residual = target
    forward = []
    for p in range(panels):
        y = mm("sij,sjc->sic", inverses[p], residual[:, :PANEL])
        forward.append(y)
        if p + 1 < panels:
            residual = residual[:, PANEL:] - mm("sij,sjc->sic", strips[p], y)
    solved = mm("sji,sjc->sic", inverses[panels - 1], forward[panels - 1])
    for p in reversed(range(panels - 1)):
        rhs = forward[p] - mm("sji,sjc->sic", strips[p], solved)
        solved = jnp.concatenate([mm("sji,sjc->sic", inverses[p], rhs), solved], axis=1)
    return solved


def pack_tiles(tiles, panels):
    pairs = tile_pairs(panels)
    off = [tiles[index] for index, (r, c) in enumerate(pairs) if r < c]
    diag = [tiles[pairs.index((p, p))] for p in range(panels)]
    sub = lax.broadcasted_iota(jnp.int32, (PANEL, PANEL), 0)
    lane = lax.broadcasted_iota(jnp.int32, (PANEL, PANEL), 1)
    packed = []
    spare = []
    for p in range(0, panels - 1, 2):
        packed.append(jnp.where(sub <= lane, diag[p], diag[p + 1]))
        spare.append(jnp.sum(jnp.where(sub == lane, diag[p + 1], 0.0), axis=0))
    if panels % 2:
        packed.append(diag[panels - 1])
    spare_rows = jnp.zeros((8, PANEL), jnp.float32)
    if spare:
        spare_rows = spare_rows.at[: len(spare)].set(jnp.stack(spare))
    return jnp.concatenate([jnp.stack(off + packed).reshape(-1, PANEL), spare_rows])


def unpack_tiles(rows, panels):
    pairs = tile_pairs(panels)
    span = rows.shape[0]
    off_count = len(pairs) - panels
    packed_count = (panels + 1) // 2
    body = rows[:, : (off_count + packed_count) * PANEL].reshape(span, off_count + packed_count, PANEL, PANEL)
    spare = rows[:, (off_count + packed_count) * PANEL :]
    sub = lax.broadcasted_iota(jnp.int32, (PANEL, PANEL), 0)
    lane = lax.broadcasted_iota(jnp.int32, (PANEL, PANEL), 1)
    diag = []
    for index in range(packed_count):
        tile = body[:, off_count + index]
        flipped = jnp.swapaxes(tile, 1, 2)
        diag.append(jnp.where(sub <= lane, tile, flipped))
        if 2 * index + 1 < panels:
            lower = jnp.where(sub > lane, tile, flipped)
            diag.append(jnp.where(sub == lane, spare[:, index][:, None, :], lower))
    out = []
    off_index = 0
    for r, c in pairs:
        if r == c:
            out.append(diag[r])
        else:
            out.append(body[:, off_index])
            off_index += 1
    return jnp.stack(out, axis=1)


def owned_layout(systems, devices, ridge_count):
    share = -(-systems // devices)
    firsts = []
    spans = []
    for device in range(devices):
        first = min(device * share, systems - 1) // ridge_count
        last = min(device * share + share - 1, systems - 1) // ridge_count
        firsts.append(first)
        spans.append(last - first + 1)
    return share, firsts, max(spans)


def shards(genotype, allele_freq, phenotype, shrinkage, owner_order):
    sample_rows = genotype.shape[0]
    devices = lax.axis_size("sample")
    me = lax.axis_index("sample")
    total_rows = sample_rows * devices
    scaled = standardize(genotype, allele_freq)
    ordered = jnp.take(phenotype, owner_order, axis=1)
    traits = ordered.shape[1]
    member_count = allele_freq.shape[0] // SNPS
    ridge_count = shrinkage.shape[0]
    panels = -(-SNPS // PANEL)
    padded_width = panels * PANEL
    tile_count = len(tile_pairs(panels))
    pair_count = FOLDS * member_count
    systems = pair_count * ridge_count
    share, firsts, span = owned_layout(systems, devices, ridge_count)
    column_sets = [scaled[:, member * SNPS : (member + 1) * SNPS] for member in range(member_count)]
    bounds = [-(-(k * total_rows) // FOLDS) for k in range(FOLDS + 1)]
    counts = jnp.array(
        [float(total_rows - (bounds[k + 1] - bounds[k])) for k in range(FOLDS)], dtype=jnp.float32
    )
    start_row = me * sample_rows
    row_ids = start_row + lax.broadcasted_iota(jnp.int32, (sample_rows,), 0)
    fold_of = row_ids * FOLDS // total_rows
    first_fold = start_row * FOLDS // total_rows
    slot_folds = [first_fold, first_fold + 1]
    slot_masks = [fold_of == slot_folds[0], fold_of == slot_folds[1]]
    picked = jnp.minimum(jnp.stack(slot_folds), FOLDS - 1)

    slot_rows = []
    for slot in range(2):
        member_rows = []
        for member in range(member_count):
            columns = jnp.pad(column_sets[member], ((0, 0), (0, padded_width - SNPS)))
            masked = jnp.where(slot_masks[slot][:, None], columns, jnp.zeros_like(columns))
            tiles = pack_tiles(tile_grams(masked, columns, panels), panels)
            cross = jnp.stack(
                [inner_products(ordered, masked[:, p * PANEL : (p + 1) * PANEL]) for p in range(panels)]
            )
            member_rows.append(jnp.concatenate([tiles.reshape(-1, PANEL), cross.reshape(-1, PANEL)]))
        slot_rows.append(jnp.stack(member_rows))
    local_rows = jnp.stack(slot_rows)

    wanted = []
    for device in range(devices):
        for offset in range(span):
            wanted.append(min(firsts[device] + offset, pair_count - 1))
    wanted_folds = jnp.array([pair // member_count for pair in wanted], jnp.int32)
    wanted_members = jnp.array([pair % member_count for pair in wanted], jnp.int32)
    member_axis = jnp.arange(member_count, dtype=jnp.int32)
    coefficient = jnp.stack(
        [
            jnp.logical_and(wanted_folds[:, None] != slot_folds[slot], wanted_members[:, None] == member_axis[None, :])
            for slot in range(2)
        ],
        axis=1,
    ).astype(jnp.float32)
    payload = None
    for slot in range(2):
        for member in range(member_count):
            term = coefficient[:, slot, member][:, None, None] * local_rows[slot, member][None]
            payload = term if payload is None else payload + term
    row_count = local_rows.shape[2]
    payload = payload.reshape(devices, span * row_count, PANEL)
    reduced = lax.psum_scatter(payload, "sample", scatter_dimension=0, tiled=True)[0]
    reduced = reduced.reshape(span, row_count, PANEL)
    split = row_count - panels * traits
    mine_grams = unpack_tiles(reduced[:, :split], panels)
    mine_crosses = reduced[:, split:].reshape(span, panels, traits, PANEL)

    owned_ids = jnp.minimum(me * share + lax.broadcasted_iota(jnp.int32, (share,), 0), systems - 1)
    pair_ids = owned_ids // ridge_count
    ridge_ids = owned_ids % ridge_count
    local_ids = pair_ids - jnp.take(jnp.array(firsts, jnp.int32), me)
    rest_tiles = jnp.take(mine_grams, local_ids, axis=0)
    rest_crosses = jnp.take(mine_crosses, local_ids, axis=0)
    chosen_counts = jnp.take(counts, pair_ids // member_count, axis=0)
    ridge = jnp.take(shrinkage, ridge_ids, axis=0)
    diag_ids = [index for index, (row_tile, col_tile) in enumerate(tile_pairs(panels)) if row_tile == col_tile]
    is_diag = jnp.zeros((tile_count,), jnp.float32).at[jnp.array(diag_ids)].set(1.0)
    position = lax.broadcasted_iota(jnp.int32, (panels, PANEL), 1) + PANEL * lax.broadcasted_iota(
        jnp.int32, (panels, PANEL), 0
    )
    padded = (position >= SNPS).astype(jnp.float32)
    pad_diag = jnp.zeros((tile_count, PANEL), jnp.float32).at[jnp.array(diag_ids)].set(padded)
    identity = jnp.eye(PANEL, dtype=jnp.float32)
    diag_add = (
        ridge[:, None, None] * is_diag[None, :, None]
        + (1.0 - ridge[:, None, None]) * pad_diag[None, :, :]
    )
    system = rest_tiles / chosen_counts[:, None, None, None] + diag_add[:, :, :, None] * identity
    target = jnp.swapaxes(rest_crosses, 2, 3).reshape(share, padded_width, traits)
    target = target / chosen_counts[:, None, None]
    solved = block_solve(system, target, panels)[:, :SNPS].astype(jnp.bfloat16)
    collected = lax.all_gather(solved, "sample", axis=0, tiled=True)
    every_weights = collected[:systems].reshape(FOLDS, member_count, ridge_count, SNPS, traits)
    weights = jnp.take(every_weights, picked, axis=0)

    def fold_predictions(member, slot_weights):
        columns = column_sets[member]
        lower = predict(columns, slot_weights[0])
        upper = predict(columns, slot_weights[1])
        return jnp.where(slot_masks[1][None, None, :], upper, lower)

    local_preds = jnp.concatenate(
        [fold_predictions(member, weights[:, member]) for member in range(member_count)], axis=1
    )
    return lax.all_to_all(local_preds, "block", split_axis=0, concat_axis=1, tiled=True)


def solution(mesh):
    in_specs = (P("sample", "block"), P("block"), P("sample", None), P(), P())
    out_specs = P("block", None, "sample")
    return jax.shard_map(shards, mesh=mesh, in_specs=in_specs, out_specs=out_specs, check_vma=False)
```

```python
import jax
import jax.numpy as jnp
from jax import lax
from jax.experimental import pallas as pl
from jax.experimental.pallas import tpu as pltpu
from jax.sharding import PartitionSpec as P

SNPS = 500
FOLDS = 5
PANEL = 128
ROW_ALIGN = 16
HIGH = lax.Precision.HIGHEST


def standardize(genotype, allele_freq):
    spread = jnp.sqrt(2.0 * allele_freq * (1.0 - allele_freq))
    return ((genotype.astype(jnp.float32) - 2.0 * allele_freq) / spread).astype(jnp.bfloat16)


def predict(columns, weights):
    stacked = jnp.transpose(weights, (2, 0, 1)).reshape(-1, weights.shape[1])
    product = lax.dot_general(
        stacked, columns, (((1,), (1,)), ((), ())), preferred_element_type=jnp.float32
    )
    return product.astype(jnp.bfloat16).reshape(
        weights.shape[2], weights.shape[0], columns.shape[0]
    )


def inner_products(left_cols, right_cols):
    return lax.dot_general(
        left_cols, right_cols, (((0,), (0,)), ((), ())), preferred_element_type=jnp.float32
    )


def tile_pairs(panels):
    pairs = []
    for row_tile in range(panels):
        for col_tile in range(row_tile, panels):
            pairs.append((row_tile, col_tile))
    return pairs


def tile_grams(left_cols, right_cols, panels):
    tile_list = []
    for row_tile, col_tile in tile_pairs(panels):
        first = left_cols[:, row_tile * PANEL : (row_tile + 1) * PANEL]
        second = right_cols[:, col_tile * PANEL : (col_tile + 1) * PANEL]
        tile_list.append(inner_products(first, second))
    return jnp.stack(tile_list)


def mm(spec, left, right):
    return jnp.einsum(spec, left, right, precision=HIGH, preferred_element_type=jnp.float32)


def inverse_factor_kernel(d_ref, w_ref, a_scr):
    count, n, _ = d_ref.shape
    a_scr[...] = d_ref[...]
    sub = lax.broadcasted_iota(jnp.int32, (n, n), 0)
    lane = lax.broadcasted_iota(jnp.int32, (n, n), 1)
    eye = jnp.where(sub == lane, 1.0, 0.0).astype(jnp.float32)
    for s in range(count):
        w_ref[s] = eye
    row_lane = lax.broadcasted_iota(jnp.int32, (1, n), 1)
    col_sub = lax.broadcasted_iota(jnp.int32, (n, 1), 0)

    def pick(row, k):
        return jnp.sum(jnp.where(row_lane == k, row, 0.0), axis=1, keepdims=True)

    def step(t, carry):
        j = 2 * t
        for s in range(count):
            a = a_scr[s]
            row0 = jnp.sum(jnp.where(sub == j, a, 0.0), axis=0, keepdims=True)
            row1 = jnp.sum(jnp.where(sub == j + 1, a, 0.0), axis=0, keepdims=True)
            col0 = jnp.sum(jnp.where(lane == j, a, 0.0), axis=1, keepdims=True)
            col1 = jnp.sum(jnp.where(lane == j + 1, a, 0.0), axis=1, keepdims=True)
            top = jnp.sqrt(pick(row0, j))
            inv_top = 1.0 / top
            off = pick(row0, j + 1) * inv_top
            bottom = jnp.sqrt(pick(row1, j + 1) - off * off)
            inv_bottom = 1.0 / bottom
            lcol0 = jnp.where(col_sub >= j, col0 * inv_top, 0.0)
            lrow0 = jnp.where(row_lane >= j, row0 * inv_top, 0.0)
            lcol1 = jnp.where(col_sub >= j + 1, (col1 - lcol0 * off) * inv_bottom, 0.0)
            lrow1 = jnp.where(row_lane >= j + 1, (row1 - lrow0 * off) * inv_bottom, 0.0)
            a_scr[s] = a - lcol0 * lrow0 - lcol1 * lrow1
            r = w_ref[s]
            x0 = jnp.sum(jnp.where(sub == j, r, 0.0), axis=0, keepdims=True) * inv_top
            w1 = jnp.sum(jnp.where(sub == j + 1, r, 0.0), axis=0, keepdims=True)
            x1 = (w1 - off * x0) * inv_bottom
            strict0 = jnp.where(col_sub > j + 1, lcol0, 0.0)
            strict1 = jnp.where(col_sub > j + 1, lcol1, 0.0)
            updated = r - strict0 * x0 - strict1 * x1
            w_ref[s] = jnp.where(sub == j, x0, jnp.where(sub == j + 1, x1, updated))
        return carry

    lax.fori_loop(0, n // 2, step, 0)


def inverse_factor(block):
    count, n, _ = block.shape
    return pl.pallas_call(
        inverse_factor_kernel,
        out_shape=jax.ShapeDtypeStruct(block.shape, jnp.float32),
        in_specs=[pl.BlockSpec(memory_space=pltpu.VMEM)],
        out_specs=pl.BlockSpec(memory_space=pltpu.VMEM),
        scratch_shapes=[pltpu.VMEM(block.shape, jnp.float32)],
        cost_estimate=pl.CostEstimate(
            flops=12 * count * n * n * n, bytes_accessed=8 * count * n * n, transcendentals=count * n
        ),
    )(block)


def block_solve(tiles, target, panels):
    pairs = tile_pairs(panels)
    bands = []
    for row_tile in range(panels):
        band = []
        for col_tile in range(panels):
            if row_tile <= col_tile:
                band.append(tiles[:, pairs.index((row_tile, col_tile))])
            else:
                band.append(jnp.swapaxes(tiles[:, pairs.index((col_tile, row_tile))], 1, 2))
        bands.append(jnp.concatenate(band, axis=2))
    trailing = jnp.concatenate(bands, axis=1)
    inverses = []
    strips = []
    for p in range(panels):
        inv = inverse_factor(trailing[:, :PANEL, :PANEL])
        inverses.append(inv)
        if p + 1 < panels:
            strip = mm("sij,skj->sik", trailing[:, PANEL:, :PANEL], inv)
            strips.append(strip)
            trailing = trailing[:, PANEL:, PANEL:] - mm("sik,sjk->sij", strip, strip)
    residual = target
    forward = []
    for p in range(panels):
        y = mm("sij,sjc->sic", inverses[p], residual[:, :PANEL])
        forward.append(y)
        if p + 1 < panels:
            residual = residual[:, PANEL:] - mm("sij,sjc->sic", strips[p], y)
    solved = mm("sji,sjc->sic", inverses[panels - 1], forward[panels - 1])
    for p in reversed(range(panels - 1)):
        rhs = forward[p] - mm("sji,sjc->sic", strips[p], solved)
        solved = jnp.concatenate([mm("sji,sjc->sic", inverses[p], rhs), solved], axis=1)
    return solved


def pack_tiles(tiles, panels):
    pairs = tile_pairs(panels)
    off = [tiles[index] for index, (r, c) in enumerate(pairs) if r < c]
    diag = [tiles[pairs.index((p, p))] for p in range(panels)]
    sub = lax.broadcasted_iota(jnp.int32, (PANEL, PANEL), 0)
    lane = lax.broadcasted_iota(jnp.int32, (PANEL, PANEL), 1)
    packed = []
    spare = []
    for p in range(0, panels - 1, 2):
        packed.append(jnp.where(sub <= lane, diag[p], diag[p + 1]))
        spare.append(jnp.sum(jnp.where(sub == lane, diag[p + 1], 0.0), axis=0))
    if panels % 2:
        packed.append(diag[panels - 1])
    spare_rows = jnp.zeros((8, PANEL), jnp.float32)
    if spare:
        spare_rows = spare_rows.at[: len(spare)].set(jnp.stack(spare))
    return jnp.concatenate([jnp.stack(off + packed).reshape(-1, PANEL), spare_rows])


def unpack_tiles(rows, panels):
    pairs = tile_pairs(panels)
    span = rows.shape[0]
    off_count = len(pairs) - panels
    packed_count = (panels + 1) // 2
    body = rows[:, : (off_count + packed_count) * PANEL].reshape(span, off_count + packed_count, PANEL, PANEL)
    spare = rows[:, (off_count + packed_count) * PANEL :]
    sub = lax.broadcasted_iota(jnp.int32, (PANEL, PANEL), 0)
    lane = lax.broadcasted_iota(jnp.int32, (PANEL, PANEL), 1)
    diag = []
    for index in range(packed_count):
        tile = body[:, off_count + index]
        flipped = jnp.swapaxes(tile, 1, 2)
        diag.append(jnp.where(sub <= lane, tile, flipped))
        if 2 * index + 1 < panels:
            lower = jnp.where(sub > lane, tile, flipped)
            diag.append(jnp.where(sub == lane, spare[:, index][:, None, :], lower))
    out = []
    off_index = 0
    for r, c in pairs:
        if r == c:
            out.append(diag[r])
        else:
            out.append(body[:, off_index])
            off_index += 1
    return jnp.stack(out, axis=1)


def owned_layout(systems, devices, ridge_count):
    share = -(-systems // devices)
    firsts = []
    spans = []
    for device in range(devices):
        first = min(device * share, systems - 1) // ridge_count
        last = min(device * share + share - 1, systems - 1) // ridge_count
        firsts.append(first)
        spans.append(last - first + 1)
    return share, firsts, max(spans)


def shards(genotype, allele_freq, phenotype, shrinkage, owner_order):
    sample_rows = genotype.shape[0]
    devices = lax.axis_size("sample")
    me = lax.axis_index("sample")
    total_rows = sample_rows * devices
    scaled = standardize(genotype, allele_freq)
    ordered = jnp.take(phenotype, owner_order, axis=1)
    traits = ordered.shape[1]
    member_count = allele_freq.shape[0] // SNPS
    ridge_count = shrinkage.shape[0]
    panels = -(-SNPS // PANEL)
    padded_width = panels * PANEL
    tile_count = len(tile_pairs(panels))
    pair_count = FOLDS * member_count
    systems = pair_count * ridge_count
    share, firsts, span = owned_layout(systems, devices, ridge_count)
    column_sets = [scaled[:, member * SNPS : (member + 1) * SNPS] for member in range(member_count)]
    bounds = [-(-(k * total_rows) // FOLDS) for k in range(FOLDS + 1)]
    counts = jnp.array(
        [float(total_rows - (bounds[k + 1] - bounds[k])) for k in range(FOLDS)], dtype=jnp.float32
    )
    start_row = me * sample_rows
    row_ids = start_row + lax.broadcasted_iota(jnp.int32, (sample_rows,), 0)
    fold_of = row_ids * FOLDS // total_rows
    first_fold = start_row * FOLDS // total_rows
    slot_folds = [first_fold, first_fold + 1]
    slot_masks = [fold_of == slot_folds[0], fold_of == slot_folds[1]]
    picked = jnp.minimum(jnp.stack(slot_folds), FOLDS - 1)

    slot_rows = []
    for slot in range(2):
        member_rows = []
        for member in range(member_count):
            columns = jnp.pad(column_sets[member], ((0, 0), (0, padded_width - SNPS)))
            masked = jnp.where(slot_masks[slot][:, None], columns, jnp.zeros_like(columns))
            tiles = pack_tiles(tile_grams(masked, columns, panels), panels)
            tiles_rows = tiles.shape[0]
            cross = jnp.stack(
                [inner_products(ordered, masked[:, p * PANEL : (p + 1) * PANEL]) for p in range(panels)]
            )
            joined = jnp.concatenate([tiles.reshape(-1, PANEL), cross.reshape(-1, PANEL)])
            joined = jnp.pad(joined, ((0, -joined.shape[0] % ROW_ALIGN), (0, 0)))
            member_rows.append(joined)
        slot_rows.append(jnp.stack(member_rows))
    local_rows = jnp.stack(slot_rows)

    wanted = []
    for device in range(devices):
        for offset in range(span):
            wanted.append(min(firsts[device] + offset, pair_count - 1))
    wanted_folds = jnp.array([pair // member_count for pair in wanted], jnp.int32)
    wanted_members = jnp.array([pair % member_count for pair in wanted], jnp.int32)
    member_axis = jnp.arange(member_count, dtype=jnp.int32)
    coefficient = jnp.stack(
        [
            jnp.logical_and(wanted_folds[:, None] != slot_folds[slot], wanted_members[:, None] == member_axis[None, :])
            for slot in range(2)
        ],
        axis=1,
    ).astype(jnp.float32)
    payload = None
    for slot in range(2):
        for member in range(member_count):
            term = coefficient[:, slot, member][:, None, None] * local_rows[slot, member][None]
            payload = term if payload is None else payload + term
    row_count = local_rows.shape[2]
    payload = payload.reshape(devices, span * row_count, PANEL)
    reduced = lax.psum_scatter(payload, "sample", scatter_dimension=0, tiled=True)[0]
    reduced = reduced.reshape(span, row_count, PANEL)
    crosses_at = tiles_rows
    mine_grams = unpack_tiles(reduced[:, :crosses_at], panels)
    mine_crosses = reduced[:, crosses_at : crosses_at + panels * traits].reshape(span, panels, traits, PANEL)

    owned_ids = jnp.minimum(me * share + lax.broadcasted_iota(jnp.int32, (share,), 0), systems - 1)
    pair_ids = owned_ids // ridge_count
    ridge_ids = owned_ids % ridge_count
    local_ids = pair_ids - jnp.take(jnp.array(firsts, jnp.int32), me)
    rest_tiles = jnp.take(mine_grams, local_ids, axis=0)
    rest_crosses = jnp.take(mine_crosses, local_ids, axis=0)
    chosen_counts = jnp.take(counts, pair_ids // member_count, axis=0)
    ridge = jnp.take(shrinkage, ridge_ids, axis=0)
    diag_ids = [index for index, (row_tile, col_tile) in enumerate(tile_pairs(panels)) if row_tile == col_tile]
    is_diag = jnp.zeros((tile_count,), jnp.float32).at[jnp.array(diag_ids)].set(1.0)
    position = lax.broadcasted_iota(jnp.int32, (panels, PANEL), 1) + PANEL * lax.broadcasted_iota(
        jnp.int32, (panels, PANEL), 0
    )
    padded = (position >= SNPS).astype(jnp.float32)
    pad_diag = jnp.zeros((tile_count, PANEL), jnp.float32).at[jnp.array(diag_ids)].set(padded)
    identity = jnp.eye(PANEL, dtype=jnp.float32)
    diag_add = (
        ridge[:, None, None] * is_diag[None, :, None]
        + (1.0 - ridge[:, None, None]) * pad_diag[None, :, :]
    )
    system = rest_tiles / chosen_counts[:, None, None, None] + diag_add[:, :, :, None] * identity
    target = jnp.swapaxes(rest_crosses, 2, 3).reshape(share, padded_width, traits)
    target = target / chosen_counts[:, None, None]
    solved = block_solve(system, target, panels)[:, :SNPS].astype(jnp.bfloat16)
    collected = lax.all_gather(solved, "sample", axis=0, tiled=True)
    every_weights = collected[:systems].reshape(FOLDS, member_count, ridge_count, SNPS, traits)
    weights = jnp.take(every_weights, picked, axis=0)

    def fold_predictions(member, slot_weights):
        columns = column_sets[member]
        lower = predict(columns, slot_weights[0])
        upper = predict(columns, slot_weights[1])
        return jnp.where(slot_masks[1][None, None, :], upper, lower)

    local_preds = jnp.concatenate(
        [fold_predictions(member, weights[:, member]) for member in range(member_count)], axis=1
    )
    return lax.all_to_all(local_preds, "block", split_axis=0, concat_axis=1, tiled=True)


def solution(mesh):
    in_specs = (P("sample", "block"), P("block"), P("sample", None), P(), P())
    out_specs = P("block", None, "sample")
    return jax.shard_map(shards, mesh=mesh, in_specs=in_specs, out_specs=out_specs, check_vma=False)
```

```python
import jax
import jax.numpy as jnp
from jax import lax
from jax.experimental import pallas as pl
from jax.experimental.pallas import tpu as pltpu
from jax.sharding import PartitionSpec as P

SNPS = 500
FOLDS = 5
PANEL = 128
ROW_ALIGN = 16
HIGH = lax.Precision.HIGHEST


def standardize(genotype, allele_freq):
    spread = jnp.sqrt(2.0 * allele_freq * (1.0 - allele_freq))
    return ((genotype.astype(jnp.float32) - 2.0 * allele_freq) / spread).astype(jnp.bfloat16)


def predict(columns, weights):
    stacked = jnp.transpose(weights, (2, 0, 1)).reshape(-1, weights.shape[1])
    product = lax.dot_general(
        stacked, columns, (((1,), (1,)), ((), ())), preferred_element_type=jnp.float32
    )
    return product.astype(jnp.bfloat16).reshape(
        weights.shape[2], weights.shape[0], columns.shape[0]
    )


def inner_products(left_cols, right_cols):
    return lax.dot_general(
        left_cols, right_cols, (((0,), (0,)), ((), ())), preferred_element_type=jnp.float32
    )


def tile_pairs(panels):
    pairs = []
    for row_tile in range(panels):
        for col_tile in range(row_tile, panels):
            pairs.append((row_tile, col_tile))
    return pairs


def tile_grams(left_cols, right_cols, panels):
    tile_list = []
    for row_tile, col_tile in tile_pairs(panels):
        first = left_cols[:, row_tile * PANEL : (row_tile + 1) * PANEL]
        second = right_cols[:, col_tile * PANEL : (col_tile + 1) * PANEL]
        tile_list.append(inner_products(first, second))
    return jnp.stack(tile_list)


def mm(spec, left, right):
    return jnp.einsum(spec, left, right, precision=HIGH, preferred_element_type=jnp.float32)


def inverse_factor_kernel(d_ref, w_ref, a_scr):
    count, n, _ = d_ref.shape
    a_scr[...] = d_ref[...]
    sub = lax.broadcasted_iota(jnp.int32, (n, n), 0)
    lane = lax.broadcasted_iota(jnp.int32, (n, n), 1)
    eye = jnp.where(sub == lane, 1.0, 0.0).astype(jnp.float32)
    for s in range(count):
        w_ref[s] = eye
    row_lane = lax.broadcasted_iota(jnp.int32, (1, n), 1)
    col_sub = lax.broadcasted_iota(jnp.int32, (n, 1), 0)

    def pick(row, k):
        return jnp.sum(jnp.where(row_lane == k, row, 0.0), axis=1, keepdims=True)

    def step(t, carry):
        j = 2 * t
        for s in range(count):
            a = a_scr[s]
            row0 = jnp.sum(jnp.where(sub == j, a, 0.0), axis=0, keepdims=True)
            row1 = jnp.sum(jnp.where(sub == j + 1, a, 0.0), axis=0, keepdims=True)
            col0 = jnp.sum(jnp.where(lane == j, a, 0.0), axis=1, keepdims=True)
            col1 = jnp.sum(jnp.where(lane == j + 1, a, 0.0), axis=1, keepdims=True)
            top = jnp.sqrt(pick(row0, j))
            inv_top = 1.0 / top
            off = pick(row0, j + 1) * inv_top
            bottom = jnp.sqrt(pick(row1, j + 1) - off * off)
            inv_bottom = 1.0 / bottom
            lcol0 = jnp.where(col_sub >= j, col0 * inv_top, 0.0)
            lrow0 = jnp.where(row_lane >= j, row0 * inv_top, 0.0)
            lcol1 = jnp.where(col_sub >= j + 1, (col1 - lcol0 * off) * inv_bottom, 0.0)
            lrow1 = jnp.where(row_lane >= j + 1, (row1 - lrow0 * off) * inv_bottom, 0.0)
            a_scr[s] = a - lcol0 * lrow0 - lcol1 * lrow1
            r = w_ref[s]
            x0 = jnp.sum(jnp.where(sub == j, r, 0.0), axis=0, keepdims=True) * inv_top
            w1 = jnp.sum(jnp.where(sub == j + 1, r, 0.0), axis=0, keepdims=True)
            x1 = (w1 - off * x0) * inv_bottom
            strict0 = jnp.where(col_sub > j + 1, lcol0, 0.0)
            strict1 = jnp.where(col_sub > j + 1, lcol1, 0.0)
            updated = r - strict0 * x0 - strict1 * x1
            w_ref[s] = jnp.where(sub == j, x0, jnp.where(sub == j + 1, x1, updated))
        return carry

    lax.fori_loop(0, n // 2, step, 0, unroll=4)


def inverse_factor(block):
    count, n, _ = block.shape
    return pl.pallas_call(
        inverse_factor_kernel,
        out_shape=jax.ShapeDtypeStruct(block.shape, jnp.float32),
        in_specs=[pl.BlockSpec(memory_space=pltpu.VMEM)],
        out_specs=pl.BlockSpec(memory_space=pltpu.VMEM),
        scratch_shapes=[pltpu.VMEM(block.shape, jnp.float32)],
        cost_estimate=pl.CostEstimate(
            flops=12 * count * n * n * n, bytes_accessed=8 * count * n * n, transcendentals=count * n
        ),
    )(block)


def block_solve(tiles, target, panels):
    pairs = tile_pairs(panels)
    bands = []
    for row_tile in range(panels):
        band = []
        for col_tile in range(panels):
            if row_tile <= col_tile:
                band.append(tiles[:, pairs.index((row_tile, col_tile))])
            else:
                band.append(jnp.swapaxes(tiles[:, pairs.index((col_tile, row_tile))], 1, 2))
        bands.append(jnp.concatenate(band, axis=2))
    trailing = jnp.concatenate(bands, axis=1)
    inverses = []
    strips = []
    for p in range(panels):
        inv = inverse_factor(trailing[:, :PANEL, :PANEL])
        inverses.append(inv)
        if p + 1 < panels:
            strip = mm("sij,skj->sik", trailing[:, PANEL:, :PANEL], inv)
            strips.append(strip)
            trailing = trailing[:, PANEL:, PANEL:] - mm("sik,sjk->sij", strip, strip)
    residual = target
    forward = []
    for p in range(panels):
        y = mm("sij,sjc->sic", inverses[p], residual[:, :PANEL])
        forward.append(y)
        if p + 1 < panels:
            residual = residual[:, PANEL:] - mm("sij,sjc->sic", strips[p], y)
    solved = mm("sji,sjc->sic", inverses[panels - 1], forward[panels - 1])
    for p in reversed(range(panels - 1)):
        rhs = forward[p] - mm("sji,sjc->sic", strips[p], solved)
        solved = jnp.concatenate([mm("sji,sjc->sic", inverses[p], rhs), solved], axis=1)
    return solved


def pack_tiles(tiles, panels):
    pairs = tile_pairs(panels)
    off = [tiles[index] for index, (r, c) in enumerate(pairs) if r < c]
    diag = [tiles[pairs.index((p, p))] for p in range(panels)]
    sub = lax.broadcasted_iota(jnp.int32, (PANEL, PANEL), 0)
    lane = lax.broadcasted_iota(jnp.int32, (PANEL, PANEL), 1)
    packed = []
    spare = []
    for p in range(0, panels - 1, 2):
        packed.append(jnp.where(sub <= lane, diag[p], diag[p + 1]))
        spare.append(jnp.sum(jnp.where(sub == lane, diag[p + 1], 0.0), axis=0))
    if panels % 2:
        packed.append(diag[panels - 1])
    spare_rows = jnp.zeros((8, PANEL), jnp.float32)
    if spare:
        spare_rows = spare_rows.at[: len(spare)].set(jnp.stack(spare))
    return jnp.concatenate([jnp.stack(off + packed).reshape(-1, PANEL), spare_rows])


def unpack_tiles(rows, panels):
    pairs = tile_pairs(panels)
    span = rows.shape[0]
    off_count = len(pairs) - panels
    packed_count = (panels + 1) // 2
    body = rows[:, : (off_count + packed_count) * PANEL].reshape(span, off_count + packed_count, PANEL, PANEL)
    spare = rows[:, (off_count + packed_count) * PANEL :]
    sub = lax.broadcasted_iota(jnp.int32, (PANEL, PANEL), 0)
    lane = lax.broadcasted_iota(jnp.int32, (PANEL, PANEL), 1)
    diag = []
    for index in range(packed_count):
        tile = body[:, off_count + index]
        flipped = jnp.swapaxes(tile, 1, 2)
        diag.append(jnp.where(sub <= lane, tile, flipped))
        if 2 * index + 1 < panels:
            lower = jnp.where(sub > lane, tile, flipped)
            diag.append(jnp.where(sub == lane, spare[:, index][:, None, :], lower))
    out = []
    off_index = 0
    for r, c in pairs:
        if r == c:
            out.append(diag[r])
        else:
            out.append(body[:, off_index])
            off_index += 1
    return jnp.stack(out, axis=1)


def owned_layout(systems, devices, ridge_count):
    share = -(-systems // devices)
    firsts = []
    spans = []
    for device in range(devices):
        first = min(device * share, systems - 1) // ridge_count
        last = min(device * share + share - 1, systems - 1) // ridge_count
        firsts.append(first)
        spans.append(last - first + 1)
    return share, firsts, max(spans)


def shards(genotype, allele_freq, phenotype, shrinkage, owner_order):
    sample_rows = genotype.shape[0]
    devices = lax.axis_size("sample")
    me = lax.axis_index("sample")
    total_rows = sample_rows * devices
    scaled = standardize(genotype, allele_freq)
    ordered = jnp.take(phenotype, owner_order, axis=1)
    traits = ordered.shape[1]
    member_count = allele_freq.shape[0] // SNPS
    ridge_count = shrinkage.shape[0]
    panels = -(-SNPS // PANEL)
    padded_width = panels * PANEL
    tile_count = len(tile_pairs(panels))
    pair_count = FOLDS * member_count
    systems = pair_count * ridge_count
    share, firsts, span = owned_layout(systems, devices, ridge_count)
    column_sets = [scaled[:, member * SNPS : (member + 1) * SNPS] for member in range(member_count)]
    bounds = [-(-(k * total_rows) // FOLDS) for k in range(FOLDS + 1)]
    counts = jnp.array(
        [float(total_rows - (bounds[k + 1] - bounds[k])) for k in range(FOLDS)], dtype=jnp.float32
    )
    start_row = me * sample_rows
    row_ids = start_row + lax.broadcasted_iota(jnp.int32, (sample_rows,), 0)
    fold_of = row_ids * FOLDS // total_rows
    first_fold = start_row * FOLDS // total_rows
    slot_folds = [first_fold, first_fold + 1]
    slot_masks = [fold_of == slot_folds[0], fold_of == slot_folds[1]]
    picked = jnp.minimum(jnp.stack(slot_folds), FOLDS - 1)

    slot_rows = []
    for slot in range(2):
        member_rows = []
        for member in range(member_count):
            columns = jnp.pad(column_sets[member], ((0, 0), (0, padded_width - SNPS)))
            masked = jnp.where(slot_masks[slot][:, None], columns, jnp.zeros_like(columns))
            tiles = pack_tiles(tile_grams(masked, columns, panels), panels)
            tiles_rows = tiles.shape[0]
            cross = jnp.stack(
                [inner_products(ordered, masked[:, p * PANEL : (p + 1) * PANEL]) for p in range(panels)]
            )
            joined = jnp.concatenate([tiles.reshape(-1, PANEL), cross.reshape(-1, PANEL)])
            joined = jnp.pad(joined, ((0, -joined.shape[0] % ROW_ALIGN), (0, 0)))
            member_rows.append(joined)
        slot_rows.append(jnp.stack(member_rows))
    local_rows = jnp.stack(slot_rows)

    wanted = []
    for device in range(devices):
        for offset in range(span):
            wanted.append(min(firsts[device] + offset, pair_count - 1))
    wanted_folds = jnp.array([pair // member_count for pair in wanted], jnp.int32)
    wanted_members = jnp.array([pair % member_count for pair in wanted], jnp.int32)
    member_axis = jnp.arange(member_count, dtype=jnp.int32)
    coefficient = jnp.stack(
        [
            jnp.logical_and(wanted_folds[:, None] != slot_folds[slot], wanted_members[:, None] == member_axis[None, :])
            for slot in range(2)
        ],
        axis=1,
    ).astype(jnp.float32)
    payload = None
    for slot in range(2):
        for member in range(member_count):
            term = coefficient[:, slot, member][:, None, None] * local_rows[slot, member][None]
            payload = term if payload is None else payload + term
    row_count = local_rows.shape[2]
    payload = payload.reshape(devices, span * row_count, PANEL)
    reduced = lax.psum_scatter(payload, "sample", scatter_dimension=0, tiled=True)[0]
    reduced = reduced.reshape(span, row_count, PANEL)
    crosses_at = tiles_rows
    mine_grams = unpack_tiles(reduced[:, :crosses_at], panels)
    mine_crosses = reduced[:, crosses_at : crosses_at + panels * traits].reshape(span, panels, traits, PANEL)

    owned_ids = jnp.minimum(me * share + lax.broadcasted_iota(jnp.int32, (share,), 0), systems - 1)
    pair_ids = owned_ids // ridge_count
    ridge_ids = owned_ids % ridge_count
    local_ids = pair_ids - jnp.take(jnp.array(firsts, jnp.int32), me)
    rest_tiles = jnp.take(mine_grams, local_ids, axis=0)
    rest_crosses = jnp.take(mine_crosses, local_ids, axis=0)
    chosen_counts = jnp.take(counts, pair_ids // member_count, axis=0)
    ridge = jnp.take(shrinkage, ridge_ids, axis=0)
    diag_ids = [index for index, (row_tile, col_tile) in enumerate(tile_pairs(panels)) if row_tile == col_tile]
    is_diag = jnp.zeros((tile_count,), jnp.float32).at[jnp.array(diag_ids)].set(1.0)
    position = lax.broadcasted_iota(jnp.int32, (panels, PANEL), 1) + PANEL * lax.broadcasted_iota(
        jnp.int32, (panels, PANEL), 0
    )
    padded = (position >= SNPS).astype(jnp.float32)
    pad_diag = jnp.zeros((tile_count, PANEL), jnp.float32).at[jnp.array(diag_ids)].set(padded)
    identity = jnp.eye(PANEL, dtype=jnp.float32)
    diag_add = (
        ridge[:, None, None] * is_diag[None, :, None]
        + (1.0 - ridge[:, None, None]) * pad_diag[None, :, :]
    )
    system = rest_tiles / chosen_counts[:, None, None, None] + diag_add[:, :, :, None] * identity
    target = jnp.swapaxes(rest_crosses, 2, 3).reshape(share, padded_width, traits)
    target = target / chosen_counts[:, None, None]
    solved = block_solve(system, target, panels)[:, :SNPS].astype(jnp.bfloat16)
    collected = lax.all_gather(solved, "sample", axis=0, tiled=True)
    every_weights = collected[:systems].reshape(FOLDS, member_count, ridge_count, SNPS, traits)
    weights = jnp.take(every_weights, picked, axis=0)

    def fold_predictions(member, slot_weights):
        columns = column_sets[member]
        lower = predict(columns, slot_weights[0])
        upper = predict(columns, slot_weights[1])
        return jnp.where(slot_masks[1][None, None, :], upper, lower)

    local_preds = jnp.concatenate(
        [fold_predictions(member, weights[:, member]) for member in range(member_count)], axis=1
    )
    return lax.all_to_all(local_preds, "block", split_axis=0, concat_axis=1, tiled=True)


def solution(mesh):
    in_specs = (P("sample", "block"), P("block"), P("sample", None), P(), P())
    out_specs = P("block", None, "sample")
    return jax.shard_map(shards, mesh=mesh, in_specs=in_specs, out_specs=out_specs, check_vma=False)
```
